256 devices in a mesh: lat: 64 (over z, x, y_lo), lon: 4 (over y_hi, core).
Axes of the slice: x: 4, y: 4 (y_hi: 2, y_lo: 2; y = y_hi * 2 + y_lo), z: 8, core: 2. Of those that a mesh axis runs over, the one named last changes fastest.
Arguments:
- weather: bfloat16 [128, 512, 512], P('lat', 'lon'), may hold values from -60 to 60
- cotangent: bfloat16 [128, 512, 512], P('lat', 'lon'), may hold values from -6 to 6
- attend_gain: float32 [512], replicated, may hold values from 0.25 to 1.75
- project_in: bfloat16 [512, 1536], replicated, may hold values from -0.176776695 to 0.176776695
- head_scale: float32 [8], replicated, may hold values from 0.5 to 48
- project_out: bfloat16 [512, 512], replicated, may hold values from -1 to 1
- convolve_gain: float32 [512], replicated, may hold values from 0.25 to 1.75
- conv_first: bfloat16 [9, 512, 512], P(None, 'lat'), may hold values from -0.09375 to 0.09375
- conv_second: bfloat16 [9, 512, 512], P(None, 'lat'), may hold values from -0.09375 to 0.09375
Outputs:
- output: bfloat16 [128, 512, 512], P('lat', 'lon')
- d_weather: bfloat16 [128, 512, 512], P('lat', 'lon')
The draws below stay inside these ranges and needn't reach their ends.
All inputs are finite; a program needn't handle non-finite values.
Results may differ from the reference program's by a relative error of at most 0.017.
The reference program's roundings to bfloat16 on the way count: a program that leaves them out, or rounds other values in their place, can miss the bound.
Values may be sent and summed in bfloat16 or wider, within the bound.
No kernel may reach another device: no remote copies, remote signals or barrier semaphores. Data moves between devices by JAX's collectives and lax.ppermute only.
A program may use at most 128 MiB of HBM per device.

```python
import math
import jax
import jax.numpy as jnp
from jax import lax

C = 512
HEADS = 8
NLAT = 128
NLON = 512


def draw_weather(key, part):
    keys = jax.random.split(key, 3)
    shape = (NLAT, NLON, C)
    lowest = math.log(0.3)
    highest = math.log(3.0)
    row_scale = jnp.exp(jax.random.uniform(keys[0], (NLAT, NLON, 1), jnp.float32, lowest, highest))
    col_scale = jnp.exp(jax.random.uniform(keys[1], (C,), jnp.float32, lowest, highest))
    field = jax.random.truncated_normal(keys[2], -6.0, 6.0, shape, jnp.float32) * row_scale * col_scale
    return field.astype(jnp.bfloat16)


def draw_project_in(key, part):
    shape = (C, 3 * C)
    base = jax.random.truncated_normal(key, -4.0, 4.0, shape, jnp.float32) / math.sqrt(C)
    return base.astype(jnp.bfloat16)


def draw_head_scale(key, part):
    return jnp.exp(jax.random.uniform(key, (HEADS,), jnp.float32, math.log(0.5), math.log(3.0)))


def block_scale(stream_key, dims, cuts, smallest, top_value):
    loudness, own = 1.0, jax.random.fold_in(stream_key, 6)
    for dim, shards_of in cuts:
        steps = jnp.exp(jax.random.uniform(jax.random.fold_in(own, dim), (shards_of,), jnp.float32, smallest / len(cuts), top_value / len(cuts)))
        loudness = loudness * jnp.repeat(steps, dims[dim] // shards_of).reshape([-1 if axis == dim else 1 for axis in range(len(dims))])
    return loudness


def centred(key, extent, scale, most, shards=(), held_as=jnp.bfloat16):
    gain = block_scale(key, extent, shards, -0.22, 0.18) if shards else 1.0
    array = jax.random.normal(key, extent, jnp.float32) * scale * gain
    return jnp.minimum(jnp.maximum(array, -most), most).astype(held_as)


def setup_inputs(seed: int = 0) -> dict:
    arg_keys = jax.random.split(jax.random.key(seed), 10)
    return {
        "weather": draw_weather(jax.random.fold_in(arg_keys[9], 71), 0),
        "cotangent": centred(arg_keys[1], (NLAT, NLON, C), 1.0, 6.0, ((0, 64), (1, 4))),
        "attend_gain": jnp.clip(1.0 + 0.15 * jax.random.normal(arg_keys[2], (C,), jnp.float32), 0.25, 1.75),
        "project_in": draw_project_in(jax.random.fold_in(arg_keys[9], 71), 0),
        "head_scale": draw_head_scale(jax.random.fold_in(arg_keys[9], 71), 0),
        "project_out": centred(arg_keys[5], (C, C), (C // 16) ** -0.5, 1.0),
        "convolve_gain": jnp.clip(1.0 + 0.15 * jax.random.normal(arg_keys[6], (C,), jnp.float32), 0.25, 1.75),
        "conv_first": centred(arg_keys[7], (9, C, C), (9 * C) ** -0.5, 0.09375, ((1, 64),)),
        "conv_second": centred(arg_keys[8], (9, C, C), (9 * C) ** -0.5, 0.09375, ((1, 64),)),
    }


def layer_norm(values, channel_gain):
    center = values - lax.optimization_barrier(jnp.mean(values, axis=-1, keepdims=True))
    spread = lax.optimization_barrier(jnp.mean(center * center, axis=-1, keepdims=True))
    return center * lax.rsqrt(spread + 1e-05) * channel_gain

def layer_norm_back(values, channel_gain, upstream):
    _, pullback = jax.vjp(lambda argument: layer_norm(argument, channel_gain), values)
    return pullback(upstream)[0]

def unit_rms(values):
    return values * lax.rsqrt(lax.optimization_barrier(jnp.mean(values * values, axis=-1, keepdims=True)) + 1e-06)

def unit_rms_back(values, upstream):
    _, pullback = jax.vjp(unit_rms, values)
    return pullback(upstream)[0]

def smooth(values):
    return jax.nn.gelu(values, approximate=True)

def smooth_slope(values):
    _, pullback = jax.vjp(smooth, values)
    return pullback(jnp.ones_like(values))[0]

def cycle_pad(values, margin):
    joined = jnp.concatenate([values[:, -margin:], values, values[:, :margin]], axis=1)
    zero_rows = jnp.zeros((margin,) + joined.shape[1:], joined.dtype)
    return jnp.concatenate([zero_rows, joined, zero_rows], axis=0)

def convolve(padded, weight, row_count, col_count, flipped):
    channels = padded.shape[-1]
    summed = jnp.zeros((row_count * col_count, weight.shape[-1]), jnp.float32)
    for offset in range(9):
        upward, sideways = divmod(offset, 3)
        if flipped:
            start_row, start_col, kernel = (2 - upward, 2 - sideways, weight[offset].T)
        else:
            start_row, start_col, kernel = (upward, sideways, weight[offset])
        window = padded[start_row:start_row + row_count, start_col:start_col + col_count].reshape(row_count * col_count, channels)
        summed = summed + jnp.dot(window, kernel, preferred_element_type=jnp.float32)
    return summed.reshape(row_count, col_count, -1)

def wide(values):
    return values.astype(jnp.float32)

def attend_row(queries, keys, values):
    scores = jnp.einsum('ihd,jhd->hij', wide(queries), wide(keys), precision=lax.Precision.HIGHEST)
    row_max = lax.optimization_barrier(jnp.max(scores, axis=-1))
    exponent = jnp.exp(scores - row_max[..., None])
    row_sum = lax.optimization_barrier(jnp.sum(exponent, axis=-1))
    weights_exp = exponent.astype(jnp.bfloat16)
    mixed = jnp.einsum('hij,jhd->ihd', wide(weights_exp), wide(values), precision=lax.Precision.HIGHEST)
    mixed = mixed / row_sum.T[..., None]
    return (mixed.astype(jnp.bfloat16), row_max, row_sum)

def attend_row_back(queries, keys, values, mixed, d_mixed, row_max, row_sum):
    scores = jnp.einsum('ihd,jhd->hij', wide(queries), wide(keys), precision=lax.Precision.HIGHEST)
    probs = jnp.exp(scores - row_max[..., None]) / row_sum[..., None]
    probs_b = probs.astype(jnp.bfloat16)
    slope = jnp.einsum('ihd,jhd->hij', wide(d_mixed), wide(values), precision=lax.Precision.HIGHEST)
    inner = lax.optimization_barrier(jnp.sum(wide(d_mixed) * wide(mixed), axis=-1)).T
    d_score = (probs * (slope - inner[..., None])).astype(jnp.bfloat16)
    d_query = jnp.einsum('hij,jhd->ihd', wide(d_score), wide(keys), precision=lax.Precision.HIGHEST)
    d_key = jnp.einsum('hij,ihd->jhd', wide(d_score), wide(queries), precision=lax.Precision.HIGHEST)
    d_value = jnp.einsum('hij,ihd->jhd', wide(probs_b), wide(d_mixed), precision=lax.Precision.HIGHEST)
    return (d_query, d_key, d_value)

def reference(weather, cotangent, attend_gain, project_in, head_scale, project_out, convolve_gain, conv_first, conv_second):
    lat_count, lon_count, channels = weather.shape
    head_dim = channels // HEADS
    source = weather.astype(jnp.float32)
    normed = layer_norm(source, attend_gain).astype(jnp.bfloat16)
    projected = jnp.dot(normed.reshape(-1, channels), project_in, preferred_element_type=jnp.float32)
    projected = projected.reshape(lat_count, lon_count, 3, HEADS, head_dim)
    query_raw = projected[:, :, 0]
    key_raw = projected[:, :, 1]
    value_raw = projected[:, :, 2]
    factor = (head_scale / math.sqrt(head_dim))[:, None]
    queries = (factor * unit_rms(query_raw)).astype(jnp.bfloat16)
    keys = unit_rms(key_raw).astype(jnp.bfloat16)
    values = value_raw.astype(jnp.bfloat16)
    mixed, row_max, row_sum = lax.map(lambda trio: attend_row(*trio), (queries, keys, values))
    attended = jnp.dot(mixed.reshape(-1, channels), project_out, preferred_element_type=jnp.float32)
    hidden = (source + attended.reshape(lat_count, lon_count, channels)).astype(jnp.bfloat16)
    hidden_wide = hidden.astype(jnp.float32)
    block_in = layer_norm(hidden_wide, convolve_gain).astype(jnp.bfloat16)
    first = convolve(cycle_pad(block_in, 1), conv_first, lat_count, lon_count, False)
    active = smooth(first).astype(jnp.bfloat16)
    second = convolve(cycle_pad(active, 1), conv_second, lat_count, lon_count, False)
    output = (hidden_wide + second).astype(jnp.bfloat16)
    d_active = convolve(cycle_pad(cotangent, 1), conv_second, lat_count, lon_count, True)
    d_first = (d_active * smooth_slope(first)).astype(jnp.bfloat16)
    d_block = convolve(cycle_pad(d_first, 1), conv_first, lat_count, lon_count, True)
    d_hidden = (cotangent.astype(jnp.float32) + layer_norm_back(hidden_wide, convolve_gain, d_block)).astype(jnp.bfloat16)
    d_mixed = jnp.dot(d_hidden.reshape(-1, channels), project_out.T, preferred_element_type=jnp.float32)
    d_mixed = d_mixed.astype(jnp.bfloat16).reshape(lat_count, lon_count, HEADS, head_dim)
    d_query, d_key, d_value = lax.map(lambda group: attend_row_back(*group), (queries, keys, values, mixed, d_mixed, row_max, row_sum))
    d_query_raw = unit_rms_back(query_raw, factor * d_query)
    d_key_raw = unit_rms_back(key_raw, d_key)
    d_proj = jnp.stack([d_query_raw, d_key_raw, d_value], axis=2).astype(jnp.bfloat16).reshape(-1, 3 * channels)
    d_normed = jnp.dot(d_proj, project_in.T, preferred_element_type=jnp.float32).reshape(lat_count, lon_count, channels)
    d_weather = (d_hidden.astype(jnp.float32) + layer_norm_back(source, attend_gain, d_normed)).astype(jnp.bfloat16)
    return (output, d_weather)
```

```python
import math

import jax
import jax.numpy as jnp
from jax import lax
from jax.sharding import Mesh, PartitionSpec as P

HEADS = 8
LAT = ("z", "x", "y_lo")
LON = ("y_hi", "core")
FINE = (8, 4, 2, 2, 2)


def ring_gather(block, axis, count):
    index = lax.axis_index(axis)
    forward = [(i, (i + 1) % count) for i in range(count)]
    backward = [(i, (i - 1) % count) for i in range(count)]
    relative = [block] + [None] * (count - 1)
    ahead, behind = block, block
    for step in range(1, count // 2 + 1):
        ahead = lax.ppermute(ahead, axis, forward)
        relative[count - step] = ahead
        if step < count - step:
            behind = lax.ppermute(behind, axis, backward)
            relative[step] = behind
    return jnp.roll(jnp.stack(relative), index, axis=0)


def gather_filters(conv_first, conv_second):
    taps, rows, width = conv_first.shape
    half = width // 2
    core = lax.axis_index("core")
    both = jnp.stack([conv_first, conv_second])
    mine = lax.dynamic_slice_in_dim(both, core * half, half, axis=3)
    for axis, count in (("y_lo", 2), ("x", 4), ("z", 8)):
        mine = ring_gather(mine, axis, count)
    mine = mine.reshape(-1, 2, taps, rows, half)
    mine = mine.transpose(1, 2, 0, 3, 4).reshape(2, taps, -1, half)
    other = lax.ppermute(mine, "core", [(0, 1), (1, 0)])
    low = jnp.where(core == 0, mine, other)
    high = jnp.where(core == 0, other, mine)
    full = jnp.concatenate([low, high], axis=-1)
    return full[0], full[1]


def with_halo(block, sides, width, periodic):
    for axis, dim in sides:
        count = lax.axis_size(axis)
        forward = [(i, i + 1) for i in range(count - 1)]
        if periodic:
            forward.append((count - 1, 0))
        backward = [(target, source) for source, target in forward]
        low = lax.ppermute(
            lax.slice_in_dim(block, block.shape[dim] - width, None, axis=dim), axis, forward
        )
        high = lax.ppermute(lax.slice_in_dim(block, 0, width, axis=dim), axis, backward)
        block = jnp.concatenate([low, block, high], axis=dim)
    return block


def layer_norm(values, channel_gain):
    center = values - jnp.mean(values, axis=-1, keepdims=True)
    spread = jnp.mean(center * center, axis=-1, keepdims=True)
    return center * lax.rsqrt(spread + 1e-05) * channel_gain


def layer_norm_back(values, channel_gain, upstream):
    _, pullback = jax.vjp(lambda argument: layer_norm(argument, channel_gain), values)
    return pullback(upstream)[0]


def unit_rms(values):
    return values * lax.rsqrt(jnp.mean(values * values, axis=-1, keepdims=True) + 1e-06)


def unit_rms_back(values, upstream):
    _, pullback = jax.vjp(unit_rms, values)
    return pullback(upstream)[0]


def smooth(values):
    return jax.nn.gelu(values, approximate=True)


def smooth_slope(values):
    _, pullback = jax.vjp(smooth, values)
    return pullback(jnp.ones_like(values))[0]


def convolve(padded, weight, row_count, col_count, flipped):
    channels = padded.shape[-1]
    summed = jnp.zeros((row_count * col_count, weight.shape[-1]), jnp.float32)
    for offset in range(9):
        upward, sideways = divmod(offset, 3)
        if flipped:
            start_row, start_col, kernel = (2 - upward, 2 - sideways, weight[offset].T)
        else:
            start_row, start_col, kernel = (upward, sideways, weight[offset])
        window = padded[
            start_row : start_row + row_count, start_col : start_col + col_count
        ].reshape(row_count * col_count, channels)
        summed = summed + jnp.dot(window, kernel, preferred_element_type=jnp.float32)
    return summed.reshape(row_count, col_count, -1)


def widen(values, margin):
    banded = with_halo(values, ((LAT, 0),), margin, False)
    return with_halo(banded, ((LON, 1),), margin, True)


def shards(
    weather,
    cotangent,
    attend_gain,
    project_in,
    head_scale,
    project_out,
    convolve_gain,
    conv_first,
    conv_second,
):
    lat_local, lon_local, channels = weather.shape
    head_dim = channels // HEADS
    filter_one, filter_two = gather_filters(conv_first, conv_second)
    source = weather.astype(jnp.float32)
    normed = layer_norm(source, attend_gain).astype(jnp.bfloat16)
    projected = jnp.dot(
        normed.reshape(-1, channels), project_in, preferred_element_type=jnp.float32
    )
    projected = projected.reshape(lat_local, lon_local, 3, HEADS, head_dim)
    query_raw = projected[:, :, 0]
    key_raw = projected[:, :, 1]
    value_raw = projected[:, :, 2]
    factor = (head_scale / math.sqrt(head_dim))[:, None]
    queries = (factor * unit_rms(query_raw)).astype(jnp.bfloat16)
    keys = unit_rms(key_raw).astype(jnp.bfloat16)
    values = value_raw.astype(jnp.bfloat16)
    key_all, value_all = (
        lax.all_gather(keys.reshape(lat_local, lon_local, channels), LON, axis=1, tiled=True),
        lax.all_gather(values.reshape(lat_local, lon_local, channels), LON, axis=1, tiled=True),
    )
    lon_total = key_all.shape[1]
    key_heads = key_all.reshape(lat_local, lon_total, HEADS, head_dim)
    value_heads = value_all.reshape(lat_local, lon_total, HEADS, head_dim)
    scores = jnp.einsum("aihd,ajhd->ahij", queries, key_heads, preferred_element_type=jnp.float32)
    row_max = jnp.max(scores, axis=-1)
    exponent = jnp.exp(scores - row_max[..., None])
    row_sum = jnp.sum(exponent, axis=-1)
    weights_exp = exponent.astype(jnp.bfloat16)
    mixed = jnp.einsum(
        "ahij,ajhd->aihd", weights_exp, value_heads, preferred_element_type=jnp.float32
    )
    mixed = (mixed / row_sum.transpose(0, 2, 1)[..., None]).astype(jnp.bfloat16)
    attended = jnp.dot(mixed.reshape(-1, channels), project_out, preferred_element_type=jnp.float32)
    hidden = (source + attended.reshape(lat_local, lon_local, channels)).astype(jnp.bfloat16)
    hidden_wide = hidden.astype(jnp.float32)
    block_in = layer_norm(hidden_wide, convolve_gain).astype(jnp.bfloat16)
    first = convolve(widen(block_in, 1), filter_one, lat_local, lon_local, False)
    active = smooth(first).astype(jnp.bfloat16)
    second = convolve(widen(active, 1), filter_two, lat_local, lon_local, False)
    output = (hidden_wide + second).astype(jnp.bfloat16)
    d_active = convolve(widen(cotangent, 1), filter_two, lat_local, lon_local, True)
    d_first = (d_active * smooth_slope(first)).astype(jnp.bfloat16)
    d_block = convolve(widen(d_first, 1), filter_one, lat_local, lon_local, True)
    d_hidden = (
        cotangent.astype(jnp.float32) + layer_norm_back(hidden_wide, convolve_gain, d_block)
    ).astype(jnp.bfloat16)
    d_mixed = jnp.dot(
        d_hidden.reshape(-1, channels), project_out.T, preferred_element_type=jnp.float32
    )
    d_mixed = d_mixed.astype(jnp.bfloat16).reshape(lat_local, lon_local, HEADS, head_dim)
    probs = exponent / row_sum[..., None]
    probs_b = probs.astype(jnp.bfloat16)
    slope = jnp.einsum("aihd,ajhd->ahij", d_mixed, value_heads, preferred_element_type=jnp.float32)
    inner = jnp.sum(d_mixed.astype(jnp.float32) * mixed.astype(jnp.float32), axis=-1).transpose(
        0, 2, 1
    )
    d_score = (probs * (slope - inner[..., None])).astype(jnp.bfloat16)
    d_query = jnp.einsum("ahij,ajhd->aihd", d_score, key_heads, preferred_element_type=jnp.float32)
    count = lon_local * lax.axis_size(LON)
    key_term = jnp.einsum("ahij,aihd->jahd", d_score, queries, preferred_element_type=jnp.float32)
    value_term = jnp.einsum("ahij,aihd->jahd", probs_b, d_mixed, preferred_element_type=jnp.float32)
    summed = (
        lax.psum_scatter(
            jnp.concatenate(
                [
                    key_term.reshape(count, lat_local, channels),
                    value_term.reshape(count, lat_local, channels),
                ],
                axis=-1,
            ).astype(jnp.bfloat16),
            LON,
            scatter_dimension=0,
            tiled=True,
        )
        .astype(jnp.float32)
        .transpose(1, 0, 2)
    )
    d_key = summed[..., :channels].reshape(lat_local, lon_local, HEADS, head_dim)
    d_value = summed[..., channels:].reshape(lat_local, lon_local, HEADS, head_dim)
    d_query_raw = unit_rms_back(query_raw, factor * d_query)
    d_key_raw = unit_rms_back(key_raw, d_key)
    d_proj = (
        jnp.stack([d_query_raw, d_key_raw, d_value], axis=2)
        .astype(jnp.bfloat16)
        .reshape(-1, 3 * channels)
    )
    d_normed = jnp.dot(d_proj, project_in.T, preferred_element_type=jnp.float32).reshape(
        lat_local, lon_local, channels
    )
    d_weather = (
        d_hidden.astype(jnp.float32) + layer_norm_back(source, attend_gain, d_normed)
    ).astype(jnp.bfloat16)
    return (output, d_weather)


def solution(mesh):
    fine = Mesh(mesh.devices.reshape(FINE), LAT + LON)
    placed = (
        P(LAT, LON, None),
        P(LAT, LON, None),
        P(),
        P(),
        P(),
        P(),
        P(),
        P(None, LAT, None),
        P(None, LAT, None),
    )
    return jax.shard_map(
        shards,
        mesh=fine,
        in_specs=placed,
        out_specs=(P(LAT, LON, None), P(LAT, LON, None)),
        check_vma=False,
    )
```

```python
import math

import jax
import jax.numpy as jnp
from jax import lax
from jax.sharding import Mesh, PartitionSpec as P

HEADS = 8
LAT = ("z", "x", "y_lo")
LON = ("y_hi", "core")
FINE = (8, 4, 2, 2, 2)


def ring_gather(block, axis, count):
    index = lax.axis_index(axis)
    forward = [(i, (i + 1) % count) for i in range(count)]
    backward = [(i, (i - 1) % count) for i in range(count)]
    relative = [block] + [None] * (count - 1)
    ahead, behind = block, block
    for step in range(1, count // 2 + 1):
        ahead = lax.ppermute(ahead, axis, forward)
        relative[count - step] = ahead
        if step < count - step:
            behind = lax.ppermute(behind, axis, backward)
            relative[step] = behind
    return jnp.roll(jnp.stack(relative), index, axis=0)


def swap(block, axis):
    return lax.ppermute(block, axis, [(0, 1), (1, 0)])


def lon_gather(block):
    core = lax.axis_index("core") == 0
    upper = lax.axis_index("y_hi") == 0
    far = swap(block, "y_hi")
    pair = jnp.stack([jnp.where(upper, block, far), jnp.where(upper, far, block)])
    other = swap(pair, "core")
    low, high = jnp.where(core, pair, other), jnp.where(core, other, pair)
    return jnp.concatenate([low[0], high[0], low[1], high[1]], axis=1)


def lon_reduce(total):
    core = lax.axis_index("core") == 0
    upper = lax.axis_index("y_hi") == 0
    blocks = total.reshape(2, 2, -1, *total.shape[1:])
    keep = jnp.where(core, blocks[:, 0], blocks[:, 1])
    send = jnp.where(core, blocks[:, 1], blocks[:, 0])
    part = keep + swap(send.astype(jnp.bfloat16), "core").astype(jnp.float32)
    keep = jnp.where(upper, part[0], part[1])
    send = jnp.where(upper, part[1], part[0])
    return keep + swap(send.astype(jnp.bfloat16), "y_hi").astype(jnp.float32)


def gather_filters(conv_first, conv_second):
    taps, rows, width = conv_first.shape
    half = width // 2
    core = lax.axis_index("core")
    both = jnp.stack([conv_first, conv_second])
    mine = lax.dynamic_slice_in_dim(both, core * half, half, axis=3)
    for axis, count in (("y_lo", 2), ("x", 4), ("z", 8)):
        mine = ring_gather(mine, axis, count)
    mine = mine.reshape(-1, 2, taps, rows, half)
    mine = mine.transpose(1, 2, 0, 3, 4).reshape(2, taps, -1, half)
    other = lax.ppermute(mine, "core", [(0, 1), (1, 0)])
    low = jnp.where(core == 0, mine, other)
    high = jnp.where(core == 0, other, mine)
    full = jnp.concatenate([low, high], axis=-1)
    return full[0], full[1]


def with_halo(block, sides, width, periodic):
    for axis, dim in sides:
        count = lax.axis_size(axis)
        forward = [(i, i + 1) for i in range(count - 1)]
        if periodic:
            forward.append((count - 1, 0))
        backward = [(target, source) for source, target in forward]
        low = lax.ppermute(
            lax.slice_in_dim(block, block.shape[dim] - width, None, axis=dim), axis, forward
        )
        high = lax.ppermute(lax.slice_in_dim(block, 0, width, axis=dim), axis, backward)
        block = jnp.concatenate([low, block, high], axis=dim)
    return block


def layer_norm(values, channel_gain):
    center = values - jnp.mean(values, axis=-1, keepdims=True)
    spread = jnp.mean(center * center, axis=-1, keepdims=True)
    return center * lax.rsqrt(spread + 1e-05) * channel_gain


def layer_norm_back(values, channel_gain, upstream):
    _, pullback = jax.vjp(lambda argument: layer_norm(argument, channel_gain), values)
    return pullback(upstream)[0]


def unit_rms(values):
    return values * lax.rsqrt(jnp.mean(values * values, axis=-1, keepdims=True) + 1e-06)


def unit_rms_back(values, upstream):
    _, pullback = jax.vjp(unit_rms, values)
    return pullback(upstream)[0]


def smooth(values):
    return jax.nn.gelu(values, approximate=True)


def smooth_slope(values):
    _, pullback = jax.vjp(smooth, values)
    return pullback(jnp.ones_like(values))[0]


def convolve(padded, weight, row_count, col_count, flipped):
    channels = padded.shape[-1]
    summed = jnp.zeros((row_count * col_count, weight.shape[-1]), jnp.float32)
    for offset in range(9):
        upward, sideways = divmod(offset, 3)
        if flipped:
            start_row, start_col, kernel = (2 - upward, 2 - sideways, weight[offset].T)
        else:
            start_row, start_col, kernel = (upward, sideways, weight[offset])
        window = padded[
            start_row : start_row + row_count, start_col : start_col + col_count
        ].reshape(row_count * col_count, channels)
        summed = summed + jnp.dot(window, kernel, preferred_element_type=jnp.float32)
    return summed.reshape(row_count, col_count, -1)


def widen(values, margin):
    banded = with_halo(values, ((LAT, 0),), margin, False)
    return with_halo(banded, ((LON, 1),), margin, True)


def shards(
    weather,
    cotangent,
    attend_gain,
    project_in,
    head_scale,
    project_out,
    convolve_gain,
    conv_first,
    conv_second,
):
    lat_local, lon_local, channels = weather.shape
    head_dim = channels // HEADS
    filter_one, filter_two = gather_filters(conv_first, conv_second)
    source = weather.astype(jnp.float32)
    normed = layer_norm(source, attend_gain).astype(jnp.bfloat16)
    projected = jnp.dot(
        normed.reshape(-1, channels), project_in, preferred_element_type=jnp.float32
    )
    projected = projected.reshape(lat_local, lon_local, 3, HEADS, head_dim)
    query_raw = projected[:, :, 0]
    key_raw = projected[:, :, 1]
    value_raw = projected[:, :, 2]
    factor = (head_scale / math.sqrt(head_dim))[:, None]
    queries = (factor * unit_rms(query_raw)).astype(jnp.bfloat16)
    keys = unit_rms(key_raw).astype(jnp.bfloat16)
    values = value_raw.astype(jnp.bfloat16)
    both_all = lon_gather(
        jnp.concatenate(
            [
                keys.reshape(lat_local, lon_local, channels),
                values.reshape(lat_local, lon_local, channels),
            ],
            axis=-1,
        )
    )
    key_all, value_all = both_all[..., :channels], both_all[..., channels:]
    lon_total = key_all.shape[1]
    key_heads = key_all.reshape(lat_local, lon_total, HEADS, head_dim)
    value_heads = value_all.reshape(lat_local, lon_total, HEADS, head_dim)
    scores = jnp.einsum("aihd,ajhd->ahij", queries, key_heads, preferred_element_type=jnp.float32)
    row_max = jnp.max(scores, axis=-1)
    exponent = jnp.exp(scores - row_max[..., None])
    row_sum = jnp.sum(exponent, axis=-1)
    weights_exp = exponent.astype(jnp.bfloat16)
    mixed = jnp.einsum(
        "ahij,ajhd->aihd", weights_exp, value_heads, preferred_element_type=jnp.float32
    )
    mixed = (mixed / row_sum.transpose(0, 2, 1)[..., None]).astype(jnp.bfloat16)
    attended = jnp.dot(mixed.reshape(-1, channels), project_out, preferred_element_type=jnp.float32)
    hidden = (source + attended.reshape(lat_local, lon_local, channels)).astype(jnp.bfloat16)
    hidden_wide = hidden.astype(jnp.float32)
    block_in = layer_norm(hidden_wide, convolve_gain).astype(jnp.bfloat16)
    first = convolve(widen(block_in, 1), filter_one, lat_local, lon_local, False)
    active = smooth(first).astype(jnp.bfloat16)
    second = convolve(widen(active, 1), filter_two, lat_local, lon_local, False)
    output = (hidden_wide + second).astype(jnp.bfloat16)
    d_active = convolve(widen(cotangent, 1), filter_two, lat_local, lon_local, True)
    d_first = (d_active * smooth_slope(first)).astype(jnp.bfloat16)
    d_block = convolve(widen(d_first, 1), filter_one, lat_local, lon_local, True)
    d_hidden = (
        cotangent.astype(jnp.float32) + layer_norm_back(hidden_wide, convolve_gain, d_block)
    ).astype(jnp.bfloat16)
    d_mixed = jnp.dot(
        d_hidden.reshape(-1, channels), project_out.T, preferred_element_type=jnp.float32
    )
    d_mixed = d_mixed.astype(jnp.bfloat16).reshape(lat_local, lon_local, HEADS, head_dim)
    probs = exponent / row_sum[..., None]
    probs_b = probs.astype(jnp.bfloat16)
    slope = jnp.einsum("aihd,ajhd->ahij", d_mixed, value_heads, preferred_element_type=jnp.float32)
    inner = jnp.sum(d_mixed.astype(jnp.float32) * mixed.astype(jnp.float32), axis=-1).transpose(
        0, 2, 1
    )
    d_score = (probs * (slope - inner[..., None])).astype(jnp.bfloat16)
    d_query = jnp.einsum("ahij,ajhd->aihd", d_score, key_heads, preferred_element_type=jnp.float32)
    count = lon_local * lax.axis_size(LON)
    key_term = jnp.einsum("ahij,aihd->jahd", d_score, queries, preferred_element_type=jnp.float32)
    value_term = jnp.einsum("ahij,aihd->jahd", probs_b, d_mixed, preferred_element_type=jnp.float32)
    summed = lon_reduce(
        jnp.concatenate(
            [
                key_term.reshape(count, lat_local, channels),
                value_term.reshape(count, lat_local, channels),
            ],
            axis=-1,
        )
    ).transpose(1, 0, 2)
    d_key = summed[..., :channels].reshape(lat_local, lon_local, HEADS, head_dim)
    d_value = summed[..., channels:].reshape(lat_local, lon_local, HEADS, head_dim)
    d_query_raw = unit_rms_back(query_raw, factor * d_query)
    d_key_raw = unit_rms_back(key_raw, d_key)
    d_proj = (
        jnp.stack([d_query_raw, d_key_raw, d_value], axis=2)
        .astype(jnp.bfloat16)
        .reshape(-1, 3 * channels)
    )
    d_normed = jnp.dot(d_proj, project_in.T, preferred_element_type=jnp.float32).reshape(
        lat_local, lon_local, channels
    )
    d_weather = (
        d_hidden.astype(jnp.float32) + layer_norm_back(source, attend_gain, d_normed)
    ).astype(jnp.bfloat16)
    return (output, d_weather)


def solution(mesh):
    fine = Mesh(mesh.devices.reshape(FINE), LAT + LON)
    placed = (
        P(LAT, LON, None),
        P(LAT, LON, None),
        P(),
        P(),
        P(),
        P(),
        P(),
        P(None, LAT, None),
        P(None, LAT, None),
    )
    return jax.shard_map(
        shards,
        mesh=fine,
        in_specs=placed,
        out_specs=(P(LAT, LON, None), P(LAT, LON, None)),
        check_vma=False,
    )
```

```python
import math

import jax
import jax.numpy as jnp
from jax import lax
from jax.sharding import Mesh, PartitionSpec as P

HEADS = 8
LAT = ("z", "x", "y_lo")
LON = ("y_hi", "core")
FINE = (8, 4, 2, 2, 2)


def ring_gather(block, axis, count, dim):
    index = lax.axis_index(axis)
    forward = [(i, (i + 1) % count) for i in range(count)]
    backward = [(i, (i - 1) % count) for i in range(count)]
    relative = [block] + [None] * (count - 1)
    ahead, behind = block, block
    for step in range(1, count // 2 + 1):
        ahead = lax.ppermute(ahead, axis, forward)
        relative[count - step] = ahead
        if step < count - step:
            behind = lax.ppermute(behind, axis, backward)
            relative[step] = behind
    return jnp.roll(jnp.stack(relative, axis=dim), index, axis=dim)


def swap(block, axis):
    return lax.ppermute(block, axis, [(0, 1), (1, 0)])


def lon_gather(block):
    core = lax.axis_index("core") == 0
    upper = lax.axis_index("y_hi") == 0
    far = swap(block, "y_hi")
    pair = jnp.stack([jnp.where(upper, block, far), jnp.where(upper, far, block)])
    other = swap(pair, "core")
    low, high = jnp.where(core, pair, other), jnp.where(core, other, pair)
    return jnp.concatenate([low[0], high[0], low[1], high[1]], axis=1)


def lon_reduce(total):
    core = lax.axis_index("core") == 0
    upper = lax.axis_index("y_hi") == 0
    blocks = total.reshape(2, 2, -1, *total.shape[1:])
    keep = jnp.where(core, blocks[:, 0], blocks[:, 1])
    send = jnp.where(core, blocks[:, 1], blocks[:, 0])
    part = keep + swap(send.astype(jnp.bfloat16), "core").astype(jnp.float32)
    keep = jnp.where(upper, part[0], part[1])
    send = jnp.where(upper, part[1], part[0])
    return keep + swap(send.astype(jnp.bfloat16), "y_hi").astype(jnp.float32)


def gather_filters(conv_first, conv_second):
    taps, rows, width = conv_first.shape
    half = width // 2
    core = lax.axis_index("core")
    both = jnp.stack([conv_first, conv_second])
    mine = lax.dynamic_slice_in_dim(both, core * half, half, axis=3)
    for axis, count in (("y_lo", 2), ("x", 4), ("z", 8)):
        mine = ring_gather(mine, axis, count, 2)
    mine = mine.reshape(2, taps, -1, half)
    other = lax.ppermute(mine, "core", [(0, 1), (1, 0)])
    return (mine[0], other[0]), (mine[1], other[1])


def with_halo(block, sides, width, periodic):
    for axis, dim in sides:
        count = lax.axis_size(axis)
        forward = [(i, i + 1) for i in range(count - 1)]
        if periodic:
            forward.append((count - 1, 0))
        backward = [(target, source) for source, target in forward]
        low = lax.ppermute(
            lax.slice_in_dim(block, block.shape[dim] - width, None, axis=dim), axis, forward
        )
        high = lax.ppermute(lax.slice_in_dim(block, 0, width, axis=dim), axis, backward)
        block = jnp.concatenate([low, block, high], axis=dim)
    return block


def layer_norm(values, channel_gain):
    center = values - jnp.mean(values, axis=-1, keepdims=True)
    spread = jnp.mean(center * center, axis=-1, keepdims=True)
    return center * lax.rsqrt(spread + 1e-05) * channel_gain


def layer_norm_back(values, channel_gain, upstream):
    _, pullback = jax.vjp(lambda argument: layer_norm(argument, channel_gain), values)
    return pullback(upstream)[0]


def unit_rms(values):
    return values * lax.rsqrt(jnp.mean(values * values, axis=-1, keepdims=True) + 1e-06)


def unit_rms_back(values, upstream):
    _, pullback = jax.vjp(unit_rms, values)
    return pullback(upstream)[0]


def smooth(values):
    return jax.nn.gelu(values, approximate=True)


def smooth_slope(values):
    _, pullback = jax.vjp(smooth, values)
    return pullback(jnp.ones_like(values))[0]


def convolve(padded, weight, row_count, col_count, flipped):
    channels = padded.shape[-1]
    mine, other = weight
    half = mine.shape[-1]
    first = lax.axis_index("core") == 0
    if flipped:
        start = lax.axis_index("core") * half
        own = lax.dynamic_slice_in_dim(padded, start, half, axis=2)
        rest = lax.dynamic_slice_in_dim(padded, half - start, half, axis=2)
        summed = jnp.zeros((row_count * col_count, channels), jnp.float32)
    else:
        summed_mine = jnp.zeros((row_count * col_count, half), jnp.float32)
        summed_other = jnp.zeros((row_count * col_count, half), jnp.float32)
    for offset in range(9):
        upward, sideways = divmod(offset, 3)
        if flipped:
            start_row, start_col = (2 - upward, 2 - sideways)
            for source, kernel in ((own, mine), (rest, other)):
                window = source[
                    start_row : start_row + row_count, start_col : start_col + col_count
                ].reshape(row_count * col_count, half)
                summed = summed + jnp.dot(
                    window, kernel[offset].T, preferred_element_type=jnp.float32
                )
        else:
            window = padded[
                upward : upward + row_count, sideways : sideways + col_count
            ].reshape(row_count * col_count, channels)
            summed_mine = summed_mine + jnp.dot(
                window, mine[offset], preferred_element_type=jnp.float32
            )
            summed_other = summed_other + jnp.dot(
                window, other[offset], preferred_element_type=jnp.float32
            )
    if not flipped:
        summed = jnp.where(
            first,
            jnp.concatenate([summed_mine, summed_other], axis=-1),
            jnp.concatenate([summed_other, summed_mine], axis=-1),
        )
    return summed.reshape(row_count, col_count, -1)


def widen(values, margin):
    banded = with_halo(values, ((LAT, 0),), margin, False)
    return with_halo(banded, ((LON, 1),), margin, True)


def shards(
    weather,
    cotangent,
    attend_gain,
    project_in,
    head_scale,
    project_out,
    convolve_gain,
    conv_first,
    conv_second,
):
    lat_local, lon_local, channels = weather.shape
    head_dim = channels // HEADS
    filter_one, filter_two = gather_filters(conv_first, conv_second)
    source = weather.astype(jnp.float32)
    normed = layer_norm(source, attend_gain).astype(jnp.bfloat16)
    projected = jnp.dot(
        normed.reshape(-1, channels), project_in, preferred_element_type=jnp.float32
    )
    projected = projected.reshape(lat_local, lon_local, 3, HEADS, head_dim)
    query_raw = projected[:, :, 0]
    key_raw = projected[:, :, 1]
    value_raw = projected[:, :, 2]
    factor = (head_scale / math.sqrt(head_dim))[:, None]
    queries = (factor * unit_rms(query_raw)).astype(jnp.bfloat16)
    keys = unit_rms(key_raw).astype(jnp.bfloat16)
    values = value_raw.astype(jnp.bfloat16)
    both_all = lon_gather(
        jnp.concatenate(
            [
                keys.reshape(lat_local, lon_local, channels),
                values.reshape(lat_local, lon_local, channels),
            ],
            axis=-1,
        )
    )
    key_all, value_all = both_all[..., :channels], both_all[..., channels:]
    lon_total = key_all.shape[1]
    key_heads = key_all.reshape(lat_local, lon_total, HEADS, head_dim)
    value_heads = value_all.reshape(lat_local, lon_total, HEADS, head_dim)
    scores = jnp.einsum("aihd,ajhd->ahij", queries, key_heads, preferred_element_type=jnp.float32)
    row_max = jnp.max(scores, axis=-1)
    exponent = jnp.exp(scores - row_max[..., None])
    row_sum = jnp.sum(exponent, axis=-1)
    weights_exp = exponent.astype(jnp.bfloat16)
    mixed = jnp.einsum(
        "ahij,ajhd->aihd", weights_exp, value_heads, preferred_element_type=jnp.float32
    )
    mixed = (mixed / row_sum.transpose(0, 2, 1)[..., None]).astype(jnp.bfloat16)
    attended = jnp.dot(mixed.reshape(-1, channels), project_out, preferred_element_type=jnp.float32)
    hidden = (source + attended.reshape(lat_local, lon_local, channels)).astype(jnp.bfloat16)
    hidden_wide = hidden.astype(jnp.float32)
    block_in = layer_norm(hidden_wide, convolve_gain).astype(jnp.bfloat16)
    paired = widen(jnp.concatenate([block_in, cotangent], axis=-1), 1)
    first = convolve(paired[..., :channels], filter_one, lat_local, lon_local, False)
    active = smooth(first).astype(jnp.bfloat16)
    second = convolve(widen(active, 1), filter_two, lat_local, lon_local, False)
    output = (hidden_wide + second).astype(jnp.bfloat16)
    d_active = convolve(paired[..., channels:], filter_two, lat_local, lon_local, True)
    d_first = (d_active * smooth_slope(first)).astype(jnp.bfloat16)
    d_block = convolve(widen(d_first, 1), filter_one, lat_local, lon_local, True)
    d_hidden = (
        cotangent.astype(jnp.float32) + layer_norm_back(hidden_wide, convolve_gain, d_block)
    ).astype(jnp.bfloat16)
    d_mixed = jnp.dot(
        d_hidden.reshape(-1, channels), project_out.T, preferred_element_type=jnp.float32
    )
    d_mixed = d_mixed.astype(jnp.bfloat16).reshape(lat_local, lon_local, HEADS, head_dim)
    probs = exponent / row_sum[..., None]
    probs_b = probs.astype(jnp.bfloat16)
    slope = jnp.einsum("aihd,ajhd->ahij", d_mixed, value_heads, preferred_element_type=jnp.float32)
    inner = jnp.sum(d_mixed.astype(jnp.float32) * mixed.astype(jnp.float32), axis=-1).transpose(
        0, 2, 1
    )
    d_score = (probs * (slope - inner[..., None])).astype(jnp.bfloat16)
    d_query = jnp.einsum("ahij,ajhd->aihd", d_score, key_heads, preferred_element_type=jnp.float32)
    count = lon_local * lax.axis_size(LON)
    key_term = jnp.einsum("ahij,aihd->jahd", d_score, queries, preferred_element_type=jnp.float32)
    value_term = jnp.einsum("ahij,aihd->jahd", probs_b, d_mixed, preferred_element_type=jnp.float32)
    summed = lon_reduce(
        jnp.concatenate(
            [
                key_term.reshape(count, lat_local, channels),
                value_term.reshape(count, lat_local, channels),
            ],
            axis=-1,
        )
    ).transpose(1, 0, 2)
    d_key = summed[..., :channels].reshape(lat_local, lon_local, HEADS, head_dim)
    d_value = summed[..., channels:].reshape(lat_local, lon_local, HEADS, head_dim)
    d_query_raw = unit_rms_back(query_raw, factor * d_query)
    d_key_raw = unit_rms_back(key_raw, d_key)
    d_proj = (
        jnp.stack([d_query_raw, d_key_raw, d_value], axis=2)
        .astype(jnp.bfloat16)
        .reshape(-1, 3 * channels)
    )
    d_normed = jnp.dot(d_proj, project_in.T, preferred_element_type=jnp.float32).reshape(
        lat_local, lon_local, channels
    )
    d_weather = (
        d_hidden.astype(jnp.float32) + layer_norm_back(source, attend_gain, d_normed)
    ).astype(jnp.bfloat16)
    return (output, d_weather)


def solution(mesh):
    fine = Mesh(mesh.devices.reshape(FINE), LAT + LON)
    placed = (
        P(LAT, LON, None),
        P(LAT, LON, None),
        P(),
        P(),
        P(),
        P(),
        P(),
        P(None, LAT, None),
        P(None, LAT, None),
    )
    return jax.shard_map(
        shards,
        mesh=fine,
        in_specs=placed,
        out_specs=(P(LAT, LON, None), P(LAT, LON, None)),
        check_vma=False,
    )
```

```python
import math

import jax
import jax.numpy as jnp
from jax import lax
from jax.sharding import Mesh, PartitionSpec as P

HEADS = 8
LAT = ("z", "x", "y_lo")
LON = ("y_hi", "core")
FINE = (8, 4, 2, 2, 2)


def ring_gather(block, axis, count, dim, ordered=True):
    index = lax.axis_index(axis)
    forward = [(i, (i + 1) % count) for i in range(count)]
    backward = [(i, (i - 1) % count) for i in range(count)]
    relative = [block] + [None] * (count - 1)
    ahead, behind = block, block
    for step in range(1, count // 2 + 1):
        ahead = lax.ppermute(ahead, axis, forward)
        relative[count - step] = ahead
        if step < count - step:
            behind = lax.ppermute(behind, axis, backward)
            relative[step] = behind
    stacked = jnp.stack(relative, axis=dim)
    return jnp.roll(stacked, index, axis=dim) if ordered else stacked


def swap(block, axis):
    return lax.ppermute(block, axis, [(0, 1), (1, 0)])


def lon_gather(block):
    core = lax.axis_index("core") == 0
    upper = lax.axis_index("y_hi") == 0
    far = swap(block, "y_hi")
    pair = jnp.stack([jnp.where(upper, block, far), jnp.where(upper, far, block)])
    other = swap(pair, "core")
    low, high = jnp.where(core, pair, other), jnp.where(core, other, pair)
    return jnp.concatenate([low[0], high[0], low[1], high[1]], axis=1)


def lon_reduce(total):
    core = lax.axis_index("core") == 0
    upper = lax.axis_index("y_hi") == 0
    blocks = total.reshape(2, 2, -1, *total.shape[1:])
    keep = jnp.where(core, blocks[:, 0], blocks[:, 1])
    send = jnp.where(core, blocks[:, 1], blocks[:, 0])
    part = keep + swap(send.astype(jnp.bfloat16), "core").astype(jnp.float32)
    keep = jnp.where(upper, part[0], part[1])
    send = jnp.where(upper, part[1], part[0])
    return keep + swap(send.astype(jnp.bfloat16), "y_hi").astype(jnp.float32)


def gather_filters(conv_first, conv_second):
    taps, rows, width = conv_first.shape
    half = width // 2
    core = lax.axis_index("core")
    both = jnp.stack([conv_first, conv_second])
    mine = lax.dynamic_slice_in_dim(both, core * half, half, axis=3)
    for axis, count in (("y_lo", 2), ("x", 4), ("z", 8)):
        mine = ring_gather(mine, axis, count, 2, axis != "z")
    mine = mine.reshape(2, taps, -1, half)
    other = lax.ppermute(mine, "core", [(0, 1), (1, 0)])
    return (mine[0], other[0]), (mine[1], other[1])


def z_turn(values, sign):
    width = values.shape[-1]
    return jnp.roll(values, sign * lax.axis_index("z") * (width // 8), axis=-1)


def with_halo(block, sides, width, periodic):
    for axis, dim in sides:
        count = lax.axis_size(axis)
        forward = [(i, i + 1) for i in range(count - 1)]
        if periodic:
            forward.append((count - 1, 0))
        backward = [(target, source) for source, target in forward]
        low = lax.ppermute(
            lax.slice_in_dim(block, block.shape[dim] - width, None, axis=dim), axis, forward
        )
        high = lax.ppermute(lax.slice_in_dim(block, 0, width, axis=dim), axis, backward)
        block = jnp.concatenate([low, block, high], axis=dim)
    return block


def layer_norm(values, channel_gain):
    center = values - jnp.mean(values, axis=-1, keepdims=True)
    spread = jnp.mean(center * center, axis=-1, keepdims=True)
    return center * lax.rsqrt(spread + 1e-05) * channel_gain


def layer_norm_back(values, channel_gain, upstream):
    _, pullback = jax.vjp(lambda argument: layer_norm(argument, channel_gain), values)
    return pullback(upstream)[0]


def unit_rms(values):
    return values * lax.rsqrt(jnp.mean(values * values, axis=-1, keepdims=True) + 1e-06)


def unit_rms_back(values, upstream):
    _, pullback = jax.vjp(unit_rms, values)
    return pullback(upstream)[0]


def smooth(values):
    return jax.nn.gelu(values, approximate=True)


def smooth_slope(values):
    _, pullback = jax.vjp(smooth, values)
    return pullback(jnp.ones_like(values))[0]


def convolve(padded, weight, row_count, col_count, flipped):
    channels = padded.shape[-1]
    mine, other = weight
    half = mine.shape[-1]
    first = lax.axis_index("core") == 0
    if not flipped:
        padded = z_turn(padded, -1)
    if flipped:
        start = lax.axis_index("core") * half
        own = lax.dynamic_slice_in_dim(padded, start, half, axis=2)
        rest = lax.dynamic_slice_in_dim(padded, half - start, half, axis=2)
        summed = jnp.zeros((row_count * col_count, channels), jnp.float32)
    else:
        summed_mine = jnp.zeros((row_count * col_count, half), jnp.float32)
        summed_other = jnp.zeros((row_count * col_count, half), jnp.float32)
    for offset in range(9):
        upward, sideways = divmod(offset, 3)
        if flipped:
            start_row, start_col = (2 - upward, 2 - sideways)
            for source, kernel in ((own, mine), (rest, other)):
                window = source[
                    start_row : start_row + row_count, start_col : start_col + col_count
                ].reshape(row_count * col_count, half)
                summed = summed + jnp.dot(
                    window, kernel[offset].T, preferred_element_type=jnp.float32
                )
        else:
            window = padded[
                upward : upward + row_count, sideways : sideways + col_count
            ].reshape(row_count * col_count, channels)
            summed_mine = summed_mine + jnp.dot(
                window, mine[offset], preferred_element_type=jnp.float32
            )
            summed_other = summed_other + jnp.dot(
                window, other[offset], preferred_element_type=jnp.float32
            )
    if not flipped:
        summed = jnp.where(
            first,
            jnp.concatenate([summed_mine, summed_other], axis=-1),
            jnp.concatenate([summed_other, summed_mine], axis=-1),
        )
    else:
        summed = z_turn(summed, 1)
    return summed.reshape(row_count, col_count, -1)


def widen(values, margin):
    banded = with_halo(values, ((LAT, 0),), margin, False)
    return with_halo(banded, ((LON, 1),), margin, True)


def shards(
    weather,
    cotangent,
    attend_gain,
    project_in,
    head_scale,
    project_out,
    convolve_gain,
    conv_first,
    conv_second,
):
    lat_local, lon_local, channels = weather.shape
    head_dim = channels // HEADS
    filter_one, filter_two = gather_filters(conv_first, conv_second)
    source = weather.astype(jnp.float32)
    normed = layer_norm(source, attend_gain).astype(jnp.bfloat16)
    projected = jnp.dot(
        normed.reshape(-1, channels), project_in, preferred_element_type=jnp.float32
    )
    projected = projected.reshape(lat_local, lon_local, 3, HEADS, head_dim)
    query_raw = projected[:, :, 0]
    key_raw = projected[:, :, 1]
    value_raw = projected[:, :, 2]
    factor = (head_scale / math.sqrt(head_dim))[:, None]
    queries = (factor * unit_rms(query_raw)).astype(jnp.bfloat16)
    keys = unit_rms(key_raw).astype(jnp.bfloat16)
    values = value_raw.astype(jnp.bfloat16)
    both_all = lon_gather(
        jnp.concatenate(
            [
                keys.reshape(lat_local, lon_local, channels),
                values.reshape(lat_local, lon_local, channels),
            ],
            axis=-1,
        )
    )
    key_all, value_all = both_all[..., :channels], both_all[..., channels:]
    lon_total = key_all.shape[1]
    key_heads = key_all.reshape(lat_local, lon_total, HEADS, head_dim)
    value_heads = value_all.reshape(lat_local, lon_total, HEADS, head_dim)
    scores = jnp.einsum("aihd,ajhd->ahij", queries, key_heads, preferred_element_type=jnp.float32)
    row_max = jnp.max(scores, axis=-1)
    exponent = jnp.exp(scores - row_max[..., None])
    row_sum = jnp.sum(exponent, axis=-1)
    weights_exp = exponent.astype(jnp.bfloat16)
    mixed = jnp.einsum(
        "ahij,ajhd->aihd", weights_exp, value_heads, preferred_element_type=jnp.float32
    )
    mixed = (mixed / row_sum.transpose(0, 2, 1)[..., None]).astype(jnp.bfloat16)
    attended = jnp.dot(mixed.reshape(-1, channels), project_out, preferred_element_type=jnp.float32)
    hidden = (source + attended.reshape(lat_local, lon_local, channels)).astype(jnp.bfloat16)
    hidden_wide = hidden.astype(jnp.float32)
    block_in = layer_norm(hidden_wide, convolve_gain).astype(jnp.bfloat16)
    paired = widen(jnp.concatenate([block_in, cotangent], axis=-1), 1)
    first = convolve(paired[..., :channels], filter_one, lat_local, lon_local, False)
    active = smooth(first).astype(jnp.bfloat16)
    second = convolve(widen(active, 1), filter_two, lat_local, lon_local, False)
    output = (hidden_wide + second).astype(jnp.bfloat16)
    d_active = convolve(paired[..., channels:], filter_two, lat_local, lon_local, True)
    d_first = (d_active * smooth_slope(first)).astype(jnp.bfloat16)
    d_block = convolve(widen(d_first, 1), filter_one, lat_local, lon_local, True)
    d_hidden = (
        cotangent.astype(jnp.float32) + layer_norm_back(hidden_wide, convolve_gain, d_block)
    ).astype(jnp.bfloat16)
    d_mixed = jnp.dot(
        d_hidden.reshape(-1, channels), project_out.T, preferred_element_type=jnp.float32
    )
    d_mixed = d_mixed.astype(jnp.bfloat16).reshape(lat_local, lon_local, HEADS, head_dim)
    probs = exponent / row_sum[..., None]
    probs_b = probs.astype(jnp.bfloat16)
    slope = jnp.einsum("aihd,ajhd->ahij", d_mixed, value_heads, preferred_element_type=jnp.float32)
    inner = jnp.sum(d_mixed.astype(jnp.float32) * mixed.astype(jnp.float32), axis=-1).transpose(
        0, 2, 1
    )
    d_score = (probs * (slope - inner[..., None])).astype(jnp.bfloat16)
    d_query = jnp.einsum("ahij,ajhd->aihd", d_score, key_heads, preferred_element_type=jnp.float32)
    count = lon_local * lax.axis_size(LON)
    key_term = jnp.einsum("ahij,aihd->jahd", d_score, queries, preferred_element_type=jnp.float32)
    value_term = jnp.einsum("ahij,aihd->jahd", probs_b, d_mixed, preferred_element_type=jnp.float32)
    summed = lon_reduce(
        jnp.concatenate(
            [
                key_term.reshape(count, lat_local, channels),
                value_term.reshape(count, lat_local, channels),
            ],
            axis=-1,
        )
    ).transpose(1, 0, 2)
    d_key = summed[..., :channels].reshape(lat_local, lon_local, HEADS, head_dim)
    d_value = summed[..., channels:].reshape(lat_local, lon_local, HEADS, head_dim)
    d_query_raw = unit_rms_back(query_raw, factor * d_query)
    d_key_raw = unit_rms_back(key_raw, d_key)
    d_proj = (
        jnp.stack([d_query_raw, d_key_raw, d_value], axis=2)
        .astype(jnp.bfloat16)
        .reshape(-1, 3 * channels)
    )
    d_normed = jnp.dot(d_proj, project_in.T, preferred_element_type=jnp.float32).reshape(
        lat_local, lon_local, channels
    )
    d_weather = (
        d_hidden.astype(jnp.float32) + layer_norm_back(source, attend_gain, d_normed)
    ).astype(jnp.bfloat16)
    return (output, d_weather)


def solution(mesh):
    fine = Mesh(mesh.devices.reshape(FINE), LAT + LON)
    placed = (
        P(LAT, LON, None),
        P(LAT, LON, None),
        P(),
        P(),
        P(),
        P(),
        P(),
        P(None, LAT, None),
        P(None, LAT, None),
    )
    return jax.shard_map(
        shards,
        mesh=fine,
        in_specs=placed,
        out_specs=(P(LAT, LON, None), P(LAT, LON, None)),
        check_vma=False,
    )
```

```python
import math

import jax
import jax.numpy as jnp
from jax import lax
from jax.sharding import Mesh, PartitionSpec as P

HEADS = 8
LAT = ("z", "x", "y_lo")
LON = ("y_hi", "core")
FINE = (8, 4, 2, 2, 2)


def ring_gather(block, axis, count, dim):
    forward = [(i, (i + 1) % count) for i in range(count)]
    backward = [(i, (i - 1) % count) for i in range(count)]
    relative = [block] + [None] * (count - 1)
    ahead, behind = block, block
    for step in range(1, count // 2 + 1):
        if step == count - step and count > 2:
            half = block.shape[-1] // 2
            near = lax.ppermute(ahead[..., :half], axis, forward)
            far = lax.ppermute(behind[..., half:], axis, backward)
            relative[step] = jnp.concatenate([near, far], axis=-1)
            continue
        ahead = lax.ppermute(ahead, axis, forward)
        relative[count - step] = ahead
        if step < count - step:
            behind = lax.ppermute(behind, axis, backward)
            relative[step] = behind
    return jnp.stack(relative, axis=dim)


def swap(block, axis):
    return lax.ppermute(block, axis, [(0, 1), (1, 0)])


def lon_gather(block):
    core = lax.axis_index("core") == 0
    upper = lax.axis_index("y_hi") == 0
    far = swap(block, "y_hi")
    pair = jnp.stack([jnp.where(upper, block, far), jnp.where(upper, far, block)])
    other = swap(pair, "core")
    low, high = jnp.where(core, pair, other), jnp.where(core, other, pair)
    return jnp.concatenate([low[0], high[0], low[1], high[1]], axis=1)


def lon_reduce(total):
    core = lax.axis_index("core") == 0
    upper = lax.axis_index("y_hi") == 0
    blocks = total.reshape(2, 2, -1, *total.shape[1:])
    keep = jnp.where(core, blocks[:, 0], blocks[:, 1])
    send = jnp.where(core, blocks[:, 1], blocks[:, 0])
    part = keep + swap(send.astype(jnp.bfloat16), "core").astype(jnp.float32)
    keep = jnp.where(upper, part[0], part[1])
    send = jnp.where(upper, part[1], part[0])
    return keep + swap(send.astype(jnp.bfloat16), "y_hi").astype(jnp.float32)


def gather_filters(conv_first, conv_second):
    taps, rows, width = conv_first.shape
    half = width // 2
    core = lax.axis_index("core")
    both = jnp.stack([conv_first, conv_second])
    mine = lax.dynamic_slice_in_dim(both, core * half, half, axis=3)
    mine = ring_gather(mine, "y_lo", 2, 2)
    mine = ring_gather(mine, "z", 8, 2)
    mine = ring_gather(mine, "x", 4, 3)
    mine = mine.reshape(2, taps, -1, half)
    other = lax.ppermute(mine, "core", [(0, 1), (1, 0)])
    return (mine[0], other[0]), (mine[1], other[1])


def turn(width, rows):
    place = jnp.arange(width)
    local = place % rows
    block = place // rows
    ring_y = block % 2
    ring_x = (block // 2) % 4
    ring_z = block // 8
    true_z = (ring_z + lax.axis_index("z")) % 8
    true_x = (ring_x + lax.axis_index("x")) % 4
    true_y = (ring_y + lax.axis_index("y_lo")) % 2
    source = ((true_z * 4 + true_x) * 2 + true_y) * rows + local
    return (place[:, None] == source[None, :]).astype(jnp.bfloat16)


def with_halo(block, sides, width, periodic):
    for axis, dim in sides:
        count = lax.axis_size(axis)
        forward = [(i, i + 1) for i in range(count - 1)]
        if periodic:
            forward.append((count - 1, 0))
        backward = [(target, source) for source, target in forward]
        low = lax.ppermute(
            lax.slice_in_dim(block, block.shape[dim] - width, None, axis=dim), axis, forward
        )
        high = lax.ppermute(lax.slice_in_dim(block, 0, width, axis=dim), axis, backward)
        block = jnp.concatenate([low, block, high], axis=dim)
    return block


def layer_norm(values, channel_gain):
    center = values - jnp.mean(values, axis=-1, keepdims=True)
    spread = jnp.mean(center * center, axis=-1, keepdims=True)
    return center * lax.rsqrt(spread + 1e-05) * channel_gain


def layer_norm_back(values, channel_gain, upstream):
    _, pullback = jax.vjp(lambda argument: layer_norm(argument, channel_gain), values)
    return pullback(upstream)[0]


def unit_rms(values):
    return values * lax.rsqrt(jnp.mean(values * values, axis=-1, keepdims=True) + 1e-06)


def unit_rms_back(values, upstream):
    _, pullback = jax.vjp(unit_rms, values)
    return pullback(upstream)[0]


def smooth(values):
    return jax.nn.gelu(values, approximate=True)


def smooth_slope(values):
    _, pullback = jax.vjp(smooth, values)
    return pullback(jnp.ones_like(values))[0]


def convolve(padded, weight, row_count, col_count, flipped):
    channels = padded.shape[-1]
    mine, other = weight
    half = mine.shape[-1]
    first = lax.axis_index("core") == 0
    rows = channels // 64
    permute = turn(channels, rows)
    if not flipped:
        padded = jnp.dot(padded, permute, preferred_element_type=jnp.float32).astype(padded.dtype)
    if flipped:
        start = lax.axis_index("core") * half
        own = lax.dynamic_slice_in_dim(padded, start, half, axis=2)
        rest = lax.dynamic_slice_in_dim(padded, half - start, half, axis=2)
        summed = jnp.zeros((row_count * col_count, channels), jnp.float32)
    else:
        summed_mine = jnp.zeros((row_count * col_count, half), jnp.float32)
        summed_other = jnp.zeros((row_count * col_count, half), jnp.float32)
    for offset in range(9):
        upward, sideways = divmod(offset, 3)
        if flipped:
            start_row, start_col = (2 - upward, 2 - sideways)
            for source, kernel in ((own, mine), (rest, other)):
                window = source[
                    start_row : start_row + row_count, start_col : start_col + col_count
                ].reshape(row_count * col_count, half)
                summed = summed + jnp.dot(
                    window, kernel[offset].T, preferred_element_type=jnp.float32
                )
        else:
            window = padded[
                upward : upward + row_count, sideways : sideways + col_count
            ].reshape(row_count * col_count, channels)
            summed_mine = summed_mine + jnp.dot(
                window, mine[offset], preferred_element_type=jnp.float32
            )
            summed_other = summed_other + jnp.dot(
                window, other[offset], preferred_element_type=jnp.float32
            )
    if not flipped:
        summed = jnp.where(
            first,
            jnp.concatenate([summed_mine, summed_other], axis=-1),
            jnp.concatenate([summed_other, summed_mine], axis=-1),
        )
    else:
        summed = jnp.dot(
            summed, permute.astype(jnp.float32).T, precision=lax.Precision.HIGHEST
        )
    return summed.reshape(row_count, col_count, -1)


def widen(values, margin):
    banded = with_halo(values, ((LAT, 0),), margin, False)
    return with_halo(banded, ((LON, 1),), margin, True)


def shards(
    weather,
    cotangent,
    attend_gain,
    project_in,
    head_scale,
    project_out,
    convolve_gain,
    conv_first,
    conv_second,
):
    lat_local, lon_local, channels = weather.shape
    head_dim = channels // HEADS
    filter_one, filter_two = gather_filters(conv_first, conv_second)
    source = weather.astype(jnp.float32)
    normed = layer_norm(source, attend_gain).astype(jnp.bfloat16)
    projected = jnp.dot(
        normed.reshape(-1, channels), project_in, preferred_element_type=jnp.float32
    )
    projected = projected.reshape(lat_local, lon_local, 3, HEADS, head_dim)
    query_raw = projected[:, :, 0]
    key_raw = projected[:, :, 1]
    value_raw = projected[:, :, 2]
    factor = (head_scale / math.sqrt(head_dim))[:, None]
    queries = (factor * unit_rms(query_raw)).astype(jnp.bfloat16)
    keys = unit_rms(key_raw).astype(jnp.bfloat16)
    values = value_raw.astype(jnp.bfloat16)
    both_all = lon_gather(
        jnp.concatenate(
            [
                keys.reshape(lat_local, lon_local, channels),
                values.reshape(lat_local, lon_local, channels),
            ],
            axis=-1,
        )
    )
    key_all, value_all = both_all[..., :channels], both_all[..., channels:]
    lon_total = key_all.shape[1]
    key_heads = key_all.reshape(lat_local, lon_total, HEADS, head_dim)
    value_heads = value_all.reshape(lat_local, lon_total, HEADS, head_dim)
    scores = jnp.einsum("aihd,ajhd->ahij", queries, key_heads, preferred_element_type=jnp.float32)
    row_max = jnp.max(scores, axis=-1)
    exponent = jnp.exp(scores - row_max[..., None])
    row_sum = jnp.sum(exponent, axis=-1)
    weights_exp = exponent.astype(jnp.bfloat16)
    mixed = jnp.einsum(
        "ahij,ajhd->aihd", weights_exp, value_heads, preferred_element_type=jnp.float32
    )
    mixed = (mixed / row_sum.transpose(0, 2, 1)[..., None]).astype(jnp.bfloat16)
    attended = jnp.dot(mixed.reshape(-1, channels), project_out, preferred_element_type=jnp.float32)
    hidden = (source + attended.reshape(lat_local, lon_local, channels)).astype(jnp.bfloat16)
    hidden_wide = hidden.astype(jnp.float32)
    block_in = layer_norm(hidden_wide, convolve_gain).astype(jnp.bfloat16)
    paired = widen(jnp.concatenate([block_in, cotangent], axis=-1), 1)
    first = convolve(paired[..., :channels], filter_one, lat_local, lon_local, False)
    active = smooth(first).astype(jnp.bfloat16)
    second = convolve(widen(active, 1), filter_two, lat_local, lon_local, False)
    output = (hidden_wide + second).astype(jnp.bfloat16)
    d_active = convolve(paired[..., channels:], filter_two, lat_local, lon_local, True)
    d_first = (d_active * smooth_slope(first)).astype(jnp.bfloat16)
    d_block = convolve(widen(d_first, 1), filter_one, lat_local, lon_local, True)
    d_hidden = (
        cotangent.astype(jnp.float32) + layer_norm_back(hidden_wide, convolve_gain, d_block)
    ).astype(jnp.bfloat16)
    d_mixed = jnp.dot(
        d_hidden.reshape(-1, channels), project_out.T, preferred_element_type=jnp.float32
    )
    d_mixed = d_mixed.astype(jnp.bfloat16).reshape(lat_local, lon_local, HEADS, head_dim)
    probs = exponent / row_sum[..., None]
    probs_b = probs.astype(jnp.bfloat16)
    slope = jnp.einsum("aihd,ajhd->ahij", d_mixed, value_heads, preferred_element_type=jnp.float32)
    inner = jnp.sum(d_mixed.astype(jnp.float32) * mixed.astype(jnp.float32), axis=-1).transpose(
        0, 2, 1
    )
    d_score = (probs * (slope - inner[..., None])).astype(jnp.bfloat16)
    d_query = jnp.einsum("ahij,ajhd->aihd", d_score, key_heads, preferred_element_type=jnp.float32)
    count = lon_local * lax.axis_size(LON)
    key_term = jnp.einsum("ahij,aihd->jahd", d_score, queries, preferred_element_type=jnp.float32)
    value_term = jnp.einsum("ahij,aihd->jahd", probs_b, d_mixed, preferred_element_type=jnp.float32)
    summed = lon_reduce(
        jnp.concatenate(
            [
                key_term.reshape(count, lat_local, channels),
                value_term.reshape(count, lat_local, channels),
            ],
            axis=-1,
        )
    ).transpose(1, 0, 2)
    d_key = summed[..., :channels].reshape(lat_local, lon_local, HEADS, head_dim)
    d_value = summed[..., channels:].reshape(lat_local, lon_local, HEADS, head_dim)
    d_query_raw = unit_rms_back(query_raw, factor * d_query)
    d_key_raw = unit_rms_back(key_raw, d_key)
    d_proj = (
        jnp.stack([d_query_raw, d_key_raw, d_value], axis=2)
        .astype(jnp.bfloat16)
        .reshape(-1, 3 * channels)
    )
    d_normed = jnp.dot(d_proj, project_in.T, preferred_element_type=jnp.float32).reshape(
        lat_local, lon_local, channels
    )
    d_weather = (
        d_hidden.astype(jnp.float32) + layer_norm_back(source, attend_gain, d_normed)
    ).astype(jnp.bfloat16)
    return (output, d_weather)


def solution(mesh):
    fine = Mesh(mesh.devices.reshape(FINE), LAT + LON)
    placed = (
        P(LAT, LON, None),
        P(LAT, LON, None),
        P(),
        P(),
        P(),
        P(),
        P(),
        P(None, LAT, None),
        P(None, LAT, None),
    )
    return jax.shard_map(
        shards,
        mesh=fine,
        in_specs=placed,
        out_specs=(P(LAT, LON, None), P(LAT, LON, None)),
        check_vma=False,
    )
```

```python
import math

import jax
import jax.numpy as jnp
from jax import lax
from jax.sharding import Mesh, PartitionSpec as P

HEADS = 8
LAT = ("z", "x", "y_lo")
LON = ("y_hi", "core")
FINE = (8, 4, 2, 2, 2)


def ring_gather(block, axis, count, dim):
    forward = [(i, (i + 1) % count) for i in range(count)]
    backward = [(i, (i - 1) % count) for i in range(count)]
    relative = [block] + [None] * (count - 1)
    ahead, behind = block, block
    for step in range(1, count // 2 + 1):
        if step == count - step and count > 2:
            half = block.shape[-1] // 2
            near = lax.ppermute(ahead[..., :half], axis, forward)
            far = lax.ppermute(behind[..., half:], axis, backward)
            relative[step] = jnp.concatenate([near, far], axis=-1)
            continue
        ahead = lax.ppermute(ahead, axis, forward)
        relative[count - step] = ahead
        if step < count - step:
            behind = lax.ppermute(behind, axis, backward)
            relative[step] = behind
    return jnp.stack(relative, axis=dim)


def swap(block, axis):
    return lax.ppermute(block, axis, [(0, 1), (1, 0)])


def lon_gather(block):
    core = lax.axis_index("core") == 0
    upper = lax.axis_index("y_hi") == 0
    far = swap(block, "y_hi")
    pair = jnp.stack([jnp.where(upper, block, far), jnp.where(upper, far, block)])
    other = swap(pair, "core")
    low, high = jnp.where(core, pair, other), jnp.where(core, other, pair)
    return jnp.concatenate([low[0], high[0], low[1], high[1]], axis=1)


def lon_reduce(total):
    core = lax.axis_index("core") == 0
    upper = lax.axis_index("y_hi") == 0
    blocks = total.reshape(total.shape[0], 2, 2, -1, *total.shape[2:])
    keep = jnp.where(core, blocks[:, :, 0], blocks[:, :, 1])
    send = jnp.where(core, blocks[:, :, 1], blocks[:, :, 0])
    part = keep + swap(send.astype(jnp.bfloat16), "core").astype(jnp.float32)
    keep = jnp.where(upper, part[:, 0], part[:, 1])
    send = jnp.where(upper, part[:, 1], part[:, 0])
    return keep + swap(send.astype(jnp.bfloat16), "y_hi").astype(jnp.float32)


def gather_filters(conv_first, conv_second):
    taps, rows, width = conv_first.shape
    half = width // 2
    core = lax.axis_index("core")
    both = jnp.stack([conv_first, conv_second])
    mine = lax.dynamic_slice_in_dim(both, core * half, half, axis=3)
    mine = ring_gather(mine, "y_lo", 2, 2)
    mine = ring_gather(mine, "z", 8, 2)
    mine = ring_gather(mine, "x", 4, 3)
    mine = mine.reshape(2, taps, -1, half)
    other = lax.ppermute(mine, "core", [(0, 1), (1, 0)])
    return (mine[0], other[0]), (mine[1], other[1])


def turn(width, rows):
    place = jnp.arange(width)
    local = place % rows
    block = place // rows
    ring_y = block % 2
    ring_x = (block // 2) % 4
    ring_z = block // 8
    true_z = (ring_z + lax.axis_index("z")) % 8
    true_x = (ring_x + lax.axis_index("x")) % 4
    true_y = (ring_y + lax.axis_index("y_lo")) % 2
    source = ((true_z * 4 + true_x) * 2 + true_y) * rows + local
    return (place[:, None] == source[None, :]).astype(jnp.bfloat16)


def with_halo(block, sides, width, periodic):
    for axis, dim in sides:
        count = lax.axis_size(axis)
        forward = [(i, i + 1) for i in range(count - 1)]
        if periodic:
            forward.append((count - 1, 0))
        backward = [(target, source) for source, target in forward]
        low = lax.ppermute(
            lax.slice_in_dim(block, block.shape[dim] - width, None, axis=dim), axis, forward
        )
        high = lax.ppermute(lax.slice_in_dim(block, 0, width, axis=dim), axis, backward)
        block = jnp.concatenate([low, block, high], axis=dim)
    return block


def layer_norm(values, channel_gain):
    center = values - jnp.mean(values, axis=-1, keepdims=True)
    spread = jnp.mean(center * center, axis=-1, keepdims=True)
    return center * lax.rsqrt(spread + 1e-05) * channel_gain


def layer_norm_back(values, channel_gain, upstream):
    _, pullback = jax.vjp(lambda argument: layer_norm(argument, channel_gain), values)
    return pullback(upstream)[0]


def unit_rms(values):
    return values * lax.rsqrt(jnp.mean(values * values, axis=-1, keepdims=True) + 1e-06)


def unit_rms_back(values, upstream):
    _, pullback = jax.vjp(unit_rms, values)
    return pullback(upstream)[0]


def smooth(values):
    return jax.nn.gelu(values, approximate=True)


def smooth_slope(values):
    _, pullback = jax.vjp(smooth, values)
    return pullback(jnp.ones_like(values))[0]


def convolve(padded, weight, row_count, col_count, flipped):
    channels = padded.shape[-1]
    mine, other = weight
    half = mine.shape[-1]
    first = lax.axis_index("core") == 0
    rows = channels // 64
    permute = turn(channels, rows)
    if not flipped:
        padded = jnp.dot(padded, permute, preferred_element_type=jnp.float32).astype(padded.dtype)
    if flipped:
        start = lax.axis_index("core") * half
        own = lax.dynamic_slice_in_dim(padded, start, half, axis=2)
        rest = lax.dynamic_slice_in_dim(padded, half - start, half, axis=2)
        summed = jnp.zeros((row_count * col_count, channels), jnp.float32)
    else:
        summed_mine = jnp.zeros((row_count * col_count, half), jnp.float32)
        summed_other = jnp.zeros((row_count * col_count, half), jnp.float32)
    for offset in range(9):
        upward, sideways = divmod(offset, 3)
        if flipped:
            start_row, start_col = (2 - upward, 2 - sideways)
            for source, kernel in ((own, mine), (rest, other)):
                window = source[
                    start_row : start_row + row_count, start_col : start_col + col_count
                ].reshape(row_count * col_count, half)
                summed = summed + jnp.dot(
                    window, kernel[offset].T, preferred_element_type=jnp.float32
                )
        else:
            window = padded[
                upward : upward + row_count, sideways : sideways + col_count
            ].reshape(row_count * col_count, channels)
            summed_mine = summed_mine + jnp.dot(
                window, mine[offset], preferred_element_type=jnp.float32
            )
            summed_other = summed_other + jnp.dot(
                window, other[offset], preferred_element_type=jnp.float32
            )
    if not flipped:
        summed = jnp.where(
            first,
            jnp.concatenate([summed_mine, summed_other], axis=-1),
            jnp.concatenate([summed_other, summed_mine], axis=-1),
        )
    else:
        summed = jnp.dot(
            summed, permute.astype(jnp.float32).T, precision=lax.Precision.HIGHEST
        )
    return summed.reshape(row_count, col_count, -1)


def widen(values, margin):
    banded = with_halo(values, ((LAT, 0),), margin, False)
    return with_halo(banded, ((LON, 1),), margin, True)


def shards(
    weather,
    cotangent,
    attend_gain,
    project_in,
    head_scale,
    project_out,
    convolve_gain,
    conv_first,
    conv_second,
):
    lat_local, lon_local, channels = weather.shape
    head_dim = channels // HEADS
    filter_one, filter_two = gather_filters(conv_first, conv_second)
    source = weather.astype(jnp.float32)
    normed = layer_norm(source, attend_gain).astype(jnp.bfloat16)
    projected = jnp.dot(
        normed.reshape(-1, channels), project_in, preferred_element_type=jnp.float32
    )
    projected = projected.reshape(lat_local, lon_local, 3, HEADS, head_dim)
    query_raw = projected[:, :, 0]
    key_raw = projected[:, :, 1]
    value_raw = projected[:, :, 2]
    factor = (head_scale / math.sqrt(head_dim))[:, None]
    queries = (factor * unit_rms(query_raw)).astype(jnp.bfloat16)
    keys = unit_rms(key_raw).astype(jnp.bfloat16)
    values = value_raw.astype(jnp.bfloat16)
    both_all = lon_gather(
        jnp.concatenate(
            [
                keys.reshape(lat_local, lon_local, channels),
                values.reshape(lat_local, lon_local, channels),
            ],
            axis=-1,
        )
    )
    key_all, value_all = both_all[..., :channels], both_all[..., channels:]
    lon_total = key_all.shape[1]
    key_heads = key_all.reshape(lat_local, lon_total, HEADS, head_dim)
    value_heads = value_all.reshape(lat_local, lon_total, HEADS, head_dim)
    scores = jnp.einsum("aihd,ajhd->ahij", queries, key_heads, preferred_element_type=jnp.float32)
    row_max = jnp.max(scores, axis=-1)
    exponent = jnp.exp(scores - row_max[..., None])
    row_sum = jnp.sum(exponent, axis=-1)
    weights_exp = exponent.astype(jnp.bfloat16)
    mixed = jnp.einsum(
        "ahij,ajhd->aihd", weights_exp, value_heads, preferred_element_type=jnp.float32
    )
    mixed = (mixed / row_sum.transpose(0, 2, 1)[..., None]).astype(jnp.bfloat16)
    attended = jnp.dot(mixed.reshape(-1, channels), project_out, preferred_element_type=jnp.float32)
    hidden = (source + attended.reshape(lat_local, lon_local, channels)).astype(jnp.bfloat16)
    hidden_wide = hidden.astype(jnp.float32)
    block_in = layer_norm(hidden_wide, convolve_gain).astype(jnp.bfloat16)
    paired = widen(jnp.concatenate([block_in, cotangent], axis=-1), 1)
    first = convolve(paired[..., :channels], filter_one, lat_local, lon_local, False)
    active = smooth(first).astype(jnp.bfloat16)
    second = convolve(widen(active, 1), filter_two, lat_local, lon_local, False)
    output = (hidden_wide + second).astype(jnp.bfloat16)
    d_active = convolve(paired[..., channels:], filter_two, lat_local, lon_local, True)
    d_first = (d_active * smooth_slope(first)).astype(jnp.bfloat16)
    d_block = convolve(widen(d_first, 1), filter_one, lat_local, lon_local, True)
    d_hidden = (
        cotangent.astype(jnp.float32) + layer_norm_back(hidden_wide, convolve_gain, d_block)
    ).astype(jnp.bfloat16)
    d_mixed = jnp.dot(
        d_hidden.reshape(-1, channels), project_out.T, preferred_element_type=jnp.float32
    )
    d_mixed = d_mixed.astype(jnp.bfloat16).reshape(lat_local, lon_local, HEADS, head_dim)
    probs = exponent / row_sum[..., None]
    probs_b = probs.astype(jnp.bfloat16)
    slope = jnp.einsum("aihd,ajhd->ahij", d_mixed, value_heads, preferred_element_type=jnp.float32)
    inner = jnp.sum(d_mixed.astype(jnp.float32) * mixed.astype(jnp.float32), axis=-1).transpose(
        0, 2, 1
    )
    d_score = (probs * (slope - inner[..., None])).astype(jnp.bfloat16)
    d_query = jnp.einsum("ahij,ajhd->aihd", d_score, key_heads, preferred_element_type=jnp.float32)
    value_term = jnp.einsum("ahij,aihd->ajhd", probs_b, d_mixed, preferred_element_type=jnp.float32)
    d_value = lon_reduce(value_term)
    key_term = jnp.einsum("ahij,aihd->ajhd", d_score, queries, preferred_element_type=jnp.float32)
    d_key = lon_reduce(key_term)
    d_query_raw = unit_rms_back(query_raw, factor * d_query)
    d_key_raw = unit_rms_back(key_raw, d_key)
    d_proj = (
        jnp.stack([d_query_raw, d_key_raw, d_value], axis=2)
        .astype(jnp.bfloat16)
        .reshape(-1, 3 * channels)
    )
    d_normed = jnp.dot(d_proj, project_in.T, preferred_element_type=jnp.float32).reshape(
        lat_local, lon_local, channels
    )
    d_weather = (
        d_hidden.astype(jnp.float32) + layer_norm_back(source, attend_gain, d_normed)
    ).astype(jnp.bfloat16)
    return (output, d_weather)


def solution(mesh):
    fine = Mesh(mesh.devices.reshape(FINE), LAT + LON)
    placed = (
        P(LAT, LON, None),
        P(LAT, LON, None),
        P(),
        P(),
        P(),
        P(),
        P(),
        P(None, LAT, None),
        P(None, LAT, None),
    )
    return jax.shard_map(
        shards,
        mesh=fine,
        in_specs=placed,
        out_specs=(P(LAT, LON, None), P(LAT, LON, None)),
        check_vma=False,
    )
```

```python
import math

import jax
import jax.numpy as jnp
from jax import lax
from jax.sharding import Mesh, PartitionSpec as P

HEADS = 8
LAT = ("z", "x", "y_lo")
LON = ("y_hi", "core")
FINE = (8, 4, 2, 2, 2)


def ring_gather(block, axis, count, dim):
    forward = [(i, (i + 1) % count) for i in range(count)]
    backward = [(i, (i - 1) % count) for i in range(count)]
    relative = [block] + [None] * (count - 1)
    ahead, behind = block, block
    for step in range(1, count // 2 + 1):
        if step == count - step and count > 2:
            half = block.shape[-1] // 2
            near = lax.ppermute(ahead[..., :half], axis, forward)
            far = lax.ppermute(behind[..., half:], axis, backward)
            relative[step] = jnp.concatenate([near, far], axis=-1)
            continue
        ahead = lax.ppermute(ahead, axis, forward)
        relative[count - step] = ahead
        if step < count - step:
            behind = lax.ppermute(behind, axis, backward)
            relative[step] = behind
    return jnp.stack(relative, axis=dim)


def swap(block, axis):
    return lax.ppermute(block, axis, [(0, 1), (1, 0)])


def lon_gather(block):
    core = lax.axis_index("core") == 0
    upper = lax.axis_index("y_hi") == 0
    far = swap(block, "y_hi")
    pair = jnp.stack([jnp.where(upper, block, far), jnp.where(upper, far, block)])
    other = swap(pair, "core")
    low, high = jnp.where(core, pair, other), jnp.where(core, other, pair)
    return jnp.concatenate([low[0], high[0], low[1], high[1]], axis=1)


def lon_reduce(total):
    core = lax.axis_index("core") == 0
    upper = lax.axis_index("y_hi") == 0
    blocks = total.reshape(2, 2, -1, *total.shape[1:])
    keep = jnp.where(core, blocks[:, 0], blocks[:, 1])
    send = jnp.where(core, blocks[:, 1], blocks[:, 0])
    part = keep + swap(send.astype(jnp.bfloat16), "core").astype(jnp.float32)
    keep = jnp.where(upper, part[0], part[1])
    send = jnp.where(upper, part[1], part[0])
    return keep + swap(send.astype(jnp.bfloat16), "y_hi").astype(jnp.float32)


def gather_filters(conv_first, conv_second):
    taps, rows, width = conv_first.shape
    half = width // 2
    core = lax.axis_index("core")
    both = jnp.stack([conv_first, conv_second])
    mine = lax.dynamic_slice_in_dim(both, core * half, half, axis=3)
    mine = ring_gather(mine, "y_lo", 2, 2)
    mine = ring_gather(mine, "z", 8, 2)
    mine = ring_gather(mine, "x", 4, 3)
    mine = mine.reshape(2, taps, -1, half)
    other = lax.ppermute(mine, "core", [(0, 1), (1, 0)])
    return (mine[0], other[0]), (mine[1], other[1])


def turn(width, rows):
    place = jnp.arange(width)
    local = place % rows
    block = place // rows
    ring_y = block % 2
    ring_x = (block // 2) % 4
    ring_z = block // 8
    true_z = (ring_z + lax.axis_index("z")) % 8
    true_x = (ring_x + lax.axis_index("x")) % 4
    true_y = (ring_y + lax.axis_index("y_lo")) % 2
    source = ((true_z * 4 + true_x) * 2 + true_y) * rows + local
    return (place[:, None] == source[None, :]).astype(jnp.bfloat16)


def with_halo(block, sides, width, periodic):
    for axis, dim in sides:
        count = lax.axis_size(axis)
        forward = [(i, i + 1) for i in range(count - 1)]
        if periodic:
            forward.append((count - 1, 0))
        backward = [(target, source) for source, target in forward]
        low = lax.ppermute(
            lax.slice_in_dim(block, block.shape[dim] - width, None, axis=dim), axis, forward
        )
        high = lax.ppermute(lax.slice_in_dim(block, 0, width, axis=dim), axis, backward)
        block = jnp.concatenate([low, block, high], axis=dim)
    return block


def layer_norm(values, channel_gain):
    center = values - jnp.mean(values, axis=-1, keepdims=True)
    spread = jnp.mean(center * center, axis=-1, keepdims=True)
    return center * lax.rsqrt(spread + 1e-05) * channel_gain


def layer_norm_back(values, channel_gain, upstream):
    _, pullback = jax.vjp(lambda argument: layer_norm(argument, channel_gain), values)
    return pullback(upstream)[0]


def unit_rms(values):
    return values * lax.rsqrt(jnp.mean(values * values, axis=-1, keepdims=True) + 1e-06)


def unit_rms_back(values, upstream):
    _, pullback = jax.vjp(unit_rms, values)
    return pullback(upstream)[0]


def smooth(values):
    return jax.nn.gelu(values, approximate=True)


def smooth_slope(values):
    _, pullback = jax.vjp(smooth, values)
    return pullback(jnp.ones_like(values))[0]


def convolve(padded, weight, row_count, col_count, flipped):
    channels = padded.shape[-1]
    mine, other = weight
    half = mine.shape[-1]
    first = lax.axis_index("core") == 0
    rows = channels // 64
    permute = turn(channels, rows)
    if not flipped:
        padded = jnp.dot(padded, permute, preferred_element_type=jnp.float32).astype(padded.dtype)
    if flipped:
        start = lax.axis_index("core") * half
        own = lax.dynamic_slice_in_dim(padded, start, half, axis=2)
        rest = lax.dynamic_slice_in_dim(padded, half - start, half, axis=2)
        summed = jnp.zeros((row_count * col_count, channels), jnp.float32)
    else:
        summed_mine = jnp.zeros((row_count * col_count, half), jnp.float32)
        summed_other = jnp.zeros((row_count * col_count, half), jnp.float32)
    for offset in range(9):
        upward, sideways = divmod(offset, 3)
        if flipped:
            start_row, start_col = (2 - upward, 2 - sideways)
            for source, kernel in ((own, mine), (rest, other)):
                window = source[
                    start_row : start_row + row_count, start_col : start_col + col_count
                ].reshape(row_count * col_count, half)
                summed = summed + jnp.dot(
                    window, kernel[offset].T, preferred_element_type=jnp.float32
                )
        else:
            window = padded[
                upward : upward + row_count, sideways : sideways + col_count
            ].reshape(row_count * col_count, channels)
            summed_mine = summed_mine + jnp.dot(
                window, mine[offset], preferred_element_type=jnp.float32
            )
            summed_other = summed_other + jnp.dot(
                window, other[offset], preferred_element_type=jnp.float32
            )
    if not flipped:
        summed = jnp.where(
            first,
            jnp.concatenate([summed_mine, summed_other], axis=-1),
            jnp.concatenate([summed_other, summed_mine], axis=-1),
        )
    else:
        summed = jnp.dot(
            summed, permute.astype(jnp.float32).T, precision=lax.Precision.HIGHEST
        )
    return summed.reshape(row_count, col_count, -1)


def widen(values, margin):
    banded = with_halo(values, ((LAT, 0),), margin, False)
    return with_halo(banded, ((LON, 1),), margin, True)


def shards(
    weather,
    cotangent,
    attend_gain,
    project_in,
    head_scale,
    project_out,
    convolve_gain,
    conv_first,
    conv_second,
):
    lat_local, lon_local, channels = weather.shape
    head_dim = channels // HEADS
    filter_one, filter_two = gather_filters(conv_first, conv_second)
    source = weather.astype(jnp.float32)
    normed = layer_norm(source, attend_gain).astype(jnp.bfloat16)
    projected = jnp.dot(
        normed.reshape(-1, channels), project_in, preferred_element_type=jnp.float32
    )
    projected = projected.reshape(lat_local, lon_local, 3, HEADS, head_dim)
    query_raw = projected[:, :, 0]
    key_raw = projected[:, :, 1]
    value_raw = projected[:, :, 2]
    factor = (head_scale / math.sqrt(head_dim))[:, None]
    queries = (factor * unit_rms(query_raw)).astype(jnp.bfloat16)
    keys = unit_rms(key_raw).astype(jnp.bfloat16)
    values = value_raw.astype(jnp.bfloat16)
    both_all = lon_gather(
        jnp.concatenate(
            [
                keys.reshape(lat_local, lon_local, channels),
                values.reshape(lat_local, lon_local, channels),
            ],
            axis=-1,
        )
    )
    key_all, value_all = both_all[..., :channels], both_all[..., channels:]
    lon_total = key_all.shape[1]
    key_heads = key_all.reshape(lat_local, lon_total, HEADS, head_dim)
    value_heads = value_all.reshape(lat_local, lon_total, HEADS, head_dim)
    scores = jnp.einsum("aihd,ajhd->ahij", queries, key_heads, preferred_element_type=jnp.float32)
    row_max = jnp.max(scores, axis=-1)
    exponent = jnp.exp(scores - row_max[..., None])
    row_sum = jnp.sum(exponent, axis=-1)
    weights_exp = exponent.astype(jnp.bfloat16)
    mixed = jnp.einsum(
        "ahij,ajhd->aihd", weights_exp, value_heads, preferred_element_type=jnp.float32
    )
    mixed = (mixed / row_sum.transpose(0, 2, 1)[..., None]).astype(jnp.bfloat16)
    attended = jnp.dot(mixed.reshape(-1, channels), project_out, preferred_element_type=jnp.float32)
    hidden = (source + attended.reshape(lat_local, lon_local, channels)).astype(jnp.bfloat16)
    hidden_wide = hidden.astype(jnp.float32)
    block_in = layer_norm(hidden_wide, convolve_gain).astype(jnp.bfloat16)
    paired = widen(jnp.concatenate([block_in, cotangent], axis=-1), 1)
    first = convolve(paired[..., :channels], filter_one, lat_local, lon_local, False)
    active = smooth(first).astype(jnp.bfloat16)
    d_active = convolve(paired[..., channels:], filter_two, lat_local, lon_local, True)
    d_first = (d_active * smooth_slope(first)).astype(jnp.bfloat16)
    later = widen(jnp.concatenate([active, d_first], axis=-1), 1)
    second = convolve(later[..., :channels], filter_two, lat_local, lon_local, False)
    output = (hidden_wide + second).astype(jnp.bfloat16)
    d_block = convolve(later[..., channels:], filter_one, lat_local, lon_local, True)
    d_hidden = (
        cotangent.astype(jnp.float32) + layer_norm_back(hidden_wide, convolve_gain, d_block)
    ).astype(jnp.bfloat16)
    d_mixed = jnp.dot(
        d_hidden.reshape(-1, channels), project_out.T, preferred_element_type=jnp.float32
    )
    d_mixed = d_mixed.astype(jnp.bfloat16).reshape(lat_local, lon_local, HEADS, head_dim)
    probs = exponent / row_sum[..., None]
    probs_b = probs.astype(jnp.bfloat16)
    slope = jnp.einsum("aihd,ajhd->ahij", d_mixed, value_heads, preferred_element_type=jnp.float32)
    inner = jnp.sum(d_mixed.astype(jnp.float32) * mixed.astype(jnp.float32), axis=-1).transpose(
        0, 2, 1
    )
    d_score = (probs * (slope - inner[..., None])).astype(jnp.bfloat16)
    d_query = jnp.einsum("ahij,ajhd->aihd", d_score, key_heads, preferred_element_type=jnp.float32)
    count = lon_local * lax.axis_size(LON)
    key_term = jnp.einsum("ahij,aihd->jahd", d_score, queries, preferred_element_type=jnp.float32)
    value_term = jnp.einsum("ahij,aihd->jahd", probs_b, d_mixed, preferred_element_type=jnp.float32)
    summed = lon_reduce(
        jnp.concatenate(
            [
                key_term.reshape(count, lat_local, channels),
                value_term.reshape(count, lat_local, channels),
            ],
            axis=-1,
        )
    ).transpose(1, 0, 2)
    d_key = summed[..., :channels].reshape(lat_local, lon_local, HEADS, head_dim)
    d_value = summed[..., channels:].reshape(lat_local, lon_local, HEADS, head_dim)
    d_query_raw = unit_rms_back(query_raw, factor * d_query)
    d_key_raw = unit_rms_back(key_raw, d_key)
    d_proj = (
        jnp.stack([d_query_raw, d_key_raw, d_value], axis=2)
        .astype(jnp.bfloat16)
        .reshape(-1, 3 * channels)
    )
    d_normed = jnp.dot(d_proj, project_in.T, preferred_element_type=jnp.float32).reshape(
        lat_local, lon_local, channels
    )
    d_weather = (
        d_hidden.astype(jnp.float32) + layer_norm_back(source, attend_gain, d_normed)
    ).astype(jnp.bfloat16)
    return (output, d_weather)


def solution(mesh):
    fine = Mesh(mesh.devices.reshape(FINE), LAT + LON)
    placed = (
        P(LAT, LON, None),
        P(LAT, LON, None),
        P(),
        P(),
        P(),
        P(),
        P(),
        P(None, LAT, None),
        P(None, LAT, None),
    )
    return jax.shard_map(
        shards,
        mesh=fine,
        in_specs=placed,
        out_specs=(P(LAT, LON, None), P(LAT, LON, None)),
        check_vma=False,
    )
```

```python
import math

import jax
import jax.numpy as jnp
from jax import lax
from jax.sharding import Mesh, PartitionSpec as P

HEADS = 8
LAT = ("z", "x", "y_lo")
LON = ("y_hi", "core")
FINE = (8, 4, 2, 2, 2)


def ring_gather(block, axis, count, dim, split=False):
    forward = [(i, (i + 1) % count) for i in range(count)]
    backward = [(i, (i - 1) % count) for i in range(count)]
    relative = [block] + [None] * (count - 1)
    ahead, behind = block, block
    for step in range(1, count // 2 + 1):
        if step == count - step and split:
            half = block.shape[-1] // 2
            near = lax.ppermute(ahead[..., :half], axis, forward)
            far = lax.ppermute(behind[..., half:], axis, backward)
            relative[step] = jnp.concatenate([near, far], axis=-1)
            continue
        ahead = lax.ppermute(ahead, axis, forward)
        relative[count - step] = ahead
        if step < count - step:
            behind = lax.ppermute(behind, axis, backward)
            relative[step] = behind
    return jnp.stack(relative, axis=dim)


def swap(block, axis):
    return lax.ppermute(block, axis, [(0, 1), (1, 0)])


def lon_gather(block):
    core = lax.axis_index("core") == 0
    upper = lax.axis_index("y_hi") == 0
    far = swap(block, "y_hi")
    pair = jnp.stack([jnp.where(upper, block, far), jnp.where(upper, far, block)])
    other = swap(pair, "core")
    low, high = jnp.where(core, pair, other), jnp.where(core, other, pair)
    return jnp.concatenate([low[0], high[0], low[1], high[1]], axis=1)


def lon_reduce(total):
    core = lax.axis_index("core") == 0
    upper = lax.axis_index("y_hi") == 0
    blocks = total.reshape(2, 2, -1, *total.shape[1:])
    keep = jnp.where(core, blocks[:, 0], blocks[:, 1])
    send = jnp.where(core, blocks[:, 1], blocks[:, 0])
    part = keep + swap(send.astype(jnp.bfloat16), "core").astype(jnp.float32)
    keep = jnp.where(upper, part[0], part[1])
    send = jnp.where(upper, part[1], part[0])
    return keep + swap(send.astype(jnp.bfloat16), "y_hi").astype(jnp.float32)


def gather_filters(conv_first, conv_second):
    taps, rows, width = conv_first.shape
    half = width // 2
    core = lax.axis_index("core")
    both = jnp.stack([conv_first, conv_second])
    mine = lax.dynamic_slice_in_dim(both, core * half, half, axis=3)
    mine = ring_gather(mine, "y_lo", 2, 2)
    mine = ring_gather(mine, "z", 8, 2)
    mine = ring_gather(mine, "x", 4, 3, True)
    mine = mine.reshape(2, taps, -1, half)
    other = lax.ppermute(mine, "core", [(0, 1), (1, 0)])
    return (mine[0], other[0]), (mine[1], other[1])


def turn(width, rows):
    place = jnp.arange(width)
    local = place % rows
    block = place // rows
    ring_y = block % 2
    ring_x = (block // 2) % 4
    ring_z = block // 8
    true_z = (ring_z + lax.axis_index("z")) % 8
    true_x = (ring_x + lax.axis_index("x")) % 4
    true_y = (ring_y + lax.axis_index("y_lo")) % 2
    source = ((true_z * 4 + true_x) * 2 + true_y) * rows + local
    return (place[:, None] == source[None, :]).astype(jnp.bfloat16)


def with_halo(block, sides, width, periodic):
    for axis, dim in sides:
        count = lax.axis_size(axis)
        forward = [(i, i + 1) for i in range(count - 1)]
        if periodic:
            forward.append((count - 1, 0))
        backward = [(target, source) for source, target in forward]
        low = lax.ppermute(
            lax.slice_in_dim(block, block.shape[dim] - width, None, axis=dim), axis, forward
        )
        high = lax.ppermute(lax.slice_in_dim(block, 0, width, axis=dim), axis, backward)
        block = jnp.concatenate([low, block, high], axis=dim)
    return block


def layer_norm(values, channel_gain):
    center = values - jnp.mean(values, axis=-1, keepdims=True)
    spread = jnp.mean(center * center, axis=-1, keepdims=True)
    return center * lax.rsqrt(spread + 1e-05) * channel_gain


def layer_norm_back(values, channel_gain, upstream):
    _, pullback = jax.vjp(lambda argument: layer_norm(argument, channel_gain), values)
    return pullback(upstream)[0]


def unit_rms(values):
    return values * lax.rsqrt(jnp.mean(values * values, axis=-1, keepdims=True) + 1e-06)


def unit_rms_back(values, upstream):
    _, pullback = jax.vjp(unit_rms, values)
    return pullback(upstream)[0]


def smooth(values):
    return jax.nn.gelu(values, approximate=True)


def smooth_slope(values):
    _, pullback = jax.vjp(smooth, values)
    return pullback(jnp.ones_like(values))[0]


def convolve(padded, weight, row_count, col_count, flipped):
    channels = padded.shape[-1]
    mine, other = weight
    half = mine.shape[-1]
    first = lax.axis_index("core") == 0
    rows = channels // 64
    permute = turn(channels, rows)
    if not flipped:
        padded = jnp.dot(padded, permute, preferred_element_type=jnp.float32).astype(padded.dtype)
    if flipped:
        start = lax.axis_index("core") * half
        own = lax.dynamic_slice_in_dim(padded, start, half, axis=2)
        rest = lax.dynamic_slice_in_dim(padded, half - start, half, axis=2)
        summed = jnp.zeros((row_count * col_count, channels), jnp.float32)
    else:
        summed_mine = jnp.zeros((row_count * col_count, half), jnp.float32)
        summed_other = jnp.zeros((row_count * col_count, half), jnp.float32)
    for offset in range(9):
        upward, sideways = divmod(offset, 3)
        if flipped:
            start_row, start_col = (2 - upward, 2 - sideways)
            for source, kernel in ((own, mine), (rest, other)):
                window = source[
                    start_row : start_row + row_count, start_col : start_col + col_count
                ].reshape(row_count * col_count, half)
                summed = summed + jnp.dot(
                    window, kernel[offset].T, preferred_element_type=jnp.float32
                )
        else:
            window = padded[
                upward : upward + row_count, sideways : sideways + col_count
            ].reshape(row_count * col_count, channels)
            summed_mine = summed_mine + jnp.dot(
                window, mine[offset], preferred_element_type=jnp.float32
            )
            summed_other = summed_other + jnp.dot(
                window, other[offset], preferred_element_type=jnp.float32
            )
    if not flipped:
        summed = jnp.where(
            first,
            jnp.concatenate([summed_mine, summed_other], axis=-1),
            jnp.concatenate([summed_other, summed_mine], axis=-1),
        )
    else:
        summed = jnp.dot(
            summed, permute.astype(jnp.float32).T, precision=lax.Precision.HIGHEST
        )
    return summed.reshape(row_count, col_count, -1)


def widen(values, margin):
    banded = with_halo(values, ((LAT, 0),), margin, False)
    return with_halo(banded, ((LON, 1),), margin, True)


def shards(
    weather,
    cotangent,
    attend_gain,
    project_in,
    head_scale,
    project_out,
    convolve_gain,
    conv_first,
    conv_second,
):
    lat_local, lon_local, channels = weather.shape
    head_dim = channels // HEADS
    filter_one, filter_two = gather_filters(conv_first, conv_second)
    source = weather.astype(jnp.float32)
    normed = layer_norm(source, attend_gain).astype(jnp.bfloat16)
    projected = jnp.dot(
        normed.reshape(-1, channels), project_in, preferred_element_type=jnp.float32
    )
    projected = projected.reshape(lat_local, lon_local, 3, HEADS, head_dim)
    query_raw = projected[:, :, 0]
    key_raw = projected[:, :, 1]
    value_raw = projected[:, :, 2]
    factor = (head_scale / math.sqrt(head_dim))[:, None]
    queries = (factor * unit_rms(query_raw)).astype(jnp.bfloat16)
    keys = unit_rms(key_raw).astype(jnp.bfloat16)
    values = value_raw.astype(jnp.bfloat16)
    both_all = lon_gather(
        jnp.concatenate(
            [
                keys.reshape(lat_local, lon_local, channels),
                values.reshape(lat_local, lon_local, channels),
            ],
            axis=-1,
        )
    )
    key_all, value_all = both_all[..., :channels], both_all[..., channels:]
    lon_total = key_all.shape[1]
    key_heads = key_all.reshape(lat_local, lon_total, HEADS, head_dim)
    value_heads = value_all.reshape(lat_local, lon_total, HEADS, head_dim)
    scores = jnp.einsum("aihd,ajhd->ahij", queries, key_heads, preferred_element_type=jnp.float32)
    row_max = jnp.max(scores, axis=-1)
    exponent = jnp.exp(scores - row_max[..., None])
    row_sum = jnp.sum(exponent, axis=-1)
    weights_exp = exponent.astype(jnp.bfloat16)
    mixed = jnp.einsum(
        "ahij,ajhd->aihd", weights_exp, value_heads, preferred_element_type=jnp.float32
    )
    mixed = (mixed / row_sum.transpose(0, 2, 1)[..., None]).astype(jnp.bfloat16)
    attended = jnp.dot(mixed.reshape(-1, channels), project_out, preferred_element_type=jnp.float32)
    hidden = (source + attended.reshape(lat_local, lon_local, channels)).astype(jnp.bfloat16)
    hidden_wide = hidden.astype(jnp.float32)
    block_in = layer_norm(hidden_wide, convolve_gain).astype(jnp.bfloat16)
    paired = widen(jnp.concatenate([block_in, cotangent], axis=-1), 1)
    first = convolve(paired[..., :channels], filter_one, lat_local, lon_local, False)
    active = smooth(first).astype(jnp.bfloat16)
    second = convolve(widen(active, 1), filter_two, lat_local, lon_local, False)
    output = (hidden_wide + second).astype(jnp.bfloat16)
    d_active = convolve(paired[..., channels:], filter_two, lat_local, lon_local, True)
    d_first = (d_active * smooth_slope(first)).astype(jnp.bfloat16)
    d_block = convolve(widen(d_first, 1), filter_one, lat_local, lon_local, True)
    d_hidden = (
        cotangent.astype(jnp.float32) + layer_norm_back(hidden_wide, convolve_gain, d_block)
    ).astype(jnp.bfloat16)
    d_mixed = jnp.dot(
        d_hidden.reshape(-1, channels), project_out.T, preferred_element_type=jnp.float32
    )
    d_mixed = d_mixed.astype(jnp.bfloat16).reshape(lat_local, lon_local, HEADS, head_dim)
    probs = exponent / row_sum[..., None]
    probs_b = probs.astype(jnp.bfloat16)
    slope = jnp.einsum("aihd,ajhd->ahij", d_mixed, value_heads, preferred_element_type=jnp.float32)
    inner = jnp.sum(d_mixed.astype(jnp.float32) * mixed.astype(jnp.float32), axis=-1).transpose(
        0, 2, 1
    )
    d_score = (probs * (slope - inner[..., None])).astype(jnp.bfloat16)
    d_query = jnp.einsum("ahij,ajhd->aihd", d_score, key_heads, preferred_element_type=jnp.float32)
    count = lon_local * lax.axis_size(LON)
    key_term = jnp.einsum("ahij,aihd->jahd", d_score, queries, preferred_element_type=jnp.float32)
    value_term = jnp.einsum("ahij,aihd->jahd", probs_b, d_mixed, preferred_element_type=jnp.float32)
    summed = lon_reduce(
        jnp.concatenate(
            [
                key_term.reshape(count, lat_local, channels),
                value_term.reshape(count, lat_local, channels),
            ],
            axis=-1,
        )
    ).transpose(1, 0, 2)
    d_key = summed[..., :channels].reshape(lat_local, lon_local, HEADS, head_dim)
    d_value = summed[..., channels:].reshape(lat_local, lon_local, HEADS, head_dim)
    d_query_raw = unit_rms_back(query_raw, factor * d_query)
    d_key_raw = unit_rms_back(key_raw, d_key)
    d_proj = (
        jnp.stack([d_query_raw, d_key_raw, d_value], axis=2)
        .astype(jnp.bfloat16)
        .reshape(-1, 3 * channels)
    )
    d_normed = jnp.dot(d_proj, project_in.T, preferred_element_type=jnp.float32).reshape(
        lat_local, lon_local, channels
    )
    d_weather = (
        d_hidden.astype(jnp.float32) + layer_norm_back(source, attend_gain, d_normed)
    ).astype(jnp.bfloat16)
    return (output, d_weather)


def solution(mesh):
    fine = Mesh(mesh.devices.reshape(FINE), LAT + LON)
    placed = (
        P(LAT, LON, None),
        P(LAT, LON, None),
        P(),
        P(),
        P(),
        P(),
        P(),
        P(None, LAT, None),
        P(None, LAT, None),
    )
    return jax.shard_map(
        shards,
        mesh=fine,
        in_specs=placed,
        out_specs=(P(LAT, LON, None), P(LAT, LON, None)),
        check_vma=False,
    )
```

```python
import math

import jax
import jax.numpy as jnp
from jax import lax
from jax.sharding import Mesh, PartitionSpec as P

HEADS = 8
LAT = ("z", "x", "y_lo")
LON = ("y_hi", "core")
FINE = (8, 4, 2, 2, 2)


def ring_gather(block, axis, count, dim, split=False):
    forward = [(i, (i + 1) % count) for i in range(count)]
    backward = [(i, (i - 1) % count) for i in range(count)]
    relative = [block] + [None] * (count - 1)
    ahead, behind = block, block
    for step in range(1, count // 2 + 1):
        if step == count - step and split:
            half = block.shape[-1] // 2
            near = lax.ppermute(ahead[..., :half], axis, forward)
            far = lax.ppermute(behind[..., half:], axis, backward)
            relative[step] = jnp.concatenate([near, far], axis=-1)
            continue
        ahead = lax.ppermute(ahead, axis, forward)
        relative[count - step] = ahead
        if step < count - step:
            behind = lax.ppermute(behind, axis, backward)
            relative[step] = behind
    return jnp.stack(relative, axis=dim)


def swap(block, axis):
    return lax.ppermute(block, axis, [(0, 1), (1, 0)])


def lon_gather(block):
    core = lax.axis_index("core") == 0
    upper = lax.axis_index("y_hi") == 0
    far = swap(block, "y_hi")
    pair = jnp.stack([jnp.where(upper, block, far), jnp.where(upper, far, block)])
    other = swap(pair, "core")
    low, high = jnp.where(core, pair, other), jnp.where(core, other, pair)
    return jnp.concatenate([low[0], high[0], low[1], high[1]], axis=1)


def lon_reduce(total):
    core = lax.axis_index("core") == 0
    upper = lax.axis_index("y_hi") == 0
    blocks = total.reshape(2, 2, -1, *total.shape[1:])
    keep = jnp.where(core, blocks[:, 0], blocks[:, 1])
    send = jnp.where(core, blocks[:, 1], blocks[:, 0])
    part = keep + swap(send.astype(jnp.bfloat16), "core").astype(jnp.float32)
    keep = jnp.where(upper, part[0], part[1])
    send = jnp.where(upper, part[1], part[0])
    return keep + swap(send.astype(jnp.bfloat16), "y_hi").astype(jnp.float32)


def gather_filters(conv_first, conv_second):
    taps, rows, width = conv_first.shape
    half = width // 2
    core = lax.axis_index("core")
    both = jnp.stack([conv_first, conv_second])
    mine = lax.dynamic_slice_in_dim(both, core * half, half, axis=3)
    mine = ring_gather(mine, "y_lo", 2, 2)
    mine = ring_gather(mine, "z", 8, 2)
    mine = ring_gather(mine, "x", 4, 3, True)
    mine = mine.reshape(2, taps, -1, half)
    other = lax.ppermute(mine, "core", [(0, 1), (1, 0)])
    return (mine[0], other[0]), (mine[1], other[1])


def turn(width, rows):
    place = jnp.arange(width)
    local = place % rows
    block = place // rows
    ring_y = block % 2
    ring_x = (block // 2) % 4
    ring_z = block // 8
    true_z = (ring_z + lax.axis_index("z")) % 8
    true_x = (ring_x + lax.axis_index("x")) % 4
    true_y = (ring_y + lax.axis_index("y_lo")) % 2
    source = ((true_z * 4 + true_x) * 2 + true_y) * rows + local
    return (place[:, None] == source[None, :]).astype(jnp.bfloat16)


def with_halo(block, sides, width, periodic):
    for axis, dim in sides:
        count = lax.axis_size(axis)
        forward = [(i, i + 1) for i in range(count - 1)]
        if periodic:
            forward.append((count - 1, 0))
        backward = [(target, source) for source, target in forward]
        low = lax.ppermute(
            lax.slice_in_dim(block, block.shape[dim] - width, None, axis=dim), axis, forward
        )
        high = lax.ppermute(lax.slice_in_dim(block, 0, width, axis=dim), axis, backward)
        block = jnp.concatenate([low, block, high], axis=dim)
    return block


def layer_norm(values, channel_gain):
    center = values - jnp.mean(values, axis=-1, keepdims=True)
    spread = jnp.mean(center * center, axis=-1, keepdims=True)
    return center * lax.rsqrt(spread + 1e-05) * channel_gain


def layer_norm_back(values, channel_gain, upstream):
    _, pullback = jax.vjp(lambda argument: layer_norm(argument, channel_gain), values)
    return pullback(upstream)[0]


def unit_rms(values):
    return values * lax.rsqrt(jnp.mean(values * values, axis=-1, keepdims=True) + 1e-06)


def unit_rms_back(values, upstream):
    _, pullback = jax.vjp(unit_rms, values)
    return pullback(upstream)[0]


def smooth(values):
    return jax.nn.gelu(values, approximate=True)


def smooth_slope(values):
    _, pullback = jax.vjp(smooth, values)
    return pullback(jnp.ones_like(values))[0]


def convolve(padded, weight, row_count, col_count, flipped):
    channels = padded.shape[-1]
    mine, other = weight
    half = mine.shape[-1]
    first = lax.axis_index("core") == 0
    rows = channels // 64
    permute = turn(channels, rows)
    if not flipped:
        padded = jnp.dot(padded, permute, preferred_element_type=jnp.float32).astype(padded.dtype)
    if flipped:
        start = lax.axis_index("core") * half
        own = lax.dynamic_slice_in_dim(padded, start, half, axis=2)
        rest = lax.dynamic_slice_in_dim(padded, half - start, half, axis=2)
        summed = jnp.zeros((row_count * col_count, channels), jnp.float32)
    else:
        windows = []
    for offset in range(9):
        upward, sideways = divmod(offset, 3)
        if flipped:
            start_row, start_col = (2 - upward, 2 - sideways)
            for source, kernel in ((own, mine), (rest, other)):
                window = source[
                    start_row : start_row + row_count, start_col : start_col + col_count
                ].reshape(row_count * col_count, half)
                summed = summed + jnp.dot(
                    window, kernel[offset].T, preferred_element_type=jnp.float32
                )
        else:
            windows.append(
                padded[upward : upward + row_count, sideways : sideways + col_count].reshape(
                    row_count * col_count, channels
                )
            )
    if not flipped:
        stacked = jnp.concatenate(windows, axis=-1)
        summed_mine = jnp.dot(
            stacked, mine.reshape(-1, half), preferred_element_type=jnp.float32
        )
        summed_other = jnp.dot(
            stacked, other.reshape(-1, half), preferred_element_type=jnp.float32
        )
    if not flipped:
        summed = jnp.where(
            first,
            jnp.concatenate([summed_mine, summed_other], axis=-1),
            jnp.concatenate([summed_other, summed_mine], axis=-1),
        )
    else:
        summed = jnp.dot(
            summed, permute.astype(jnp.float32).T, precision=lax.Precision.HIGHEST
        )
    return summed.reshape(row_count, col_count, -1)


def widen(values, margin):
    banded = with_halo(values, ((LAT, 0),), margin, False)
    return with_halo(banded, ((LON, 1),), margin, True)


def shards(
    weather,
    cotangent,
    attend_gain,
    project_in,
    head_scale,
    project_out,
    convolve_gain,
    conv_first,
    conv_second,
):
    lat_local, lon_local, channels = weather.shape
    head_dim = channels // HEADS
    filter_one, filter_two = gather_filters(conv_first, conv_second)
    source = weather.astype(jnp.float32)
    normed = layer_norm(source, attend_gain).astype(jnp.bfloat16)
    projected = jnp.dot(
        normed.reshape(-1, channels), project_in, preferred_element_type=jnp.float32
    )
    projected = projected.reshape(lat_local, lon_local, 3, HEADS, head_dim)
    query_raw = projected[:, :, 0]
    key_raw = projected[:, :, 1]
    value_raw = projected[:, :, 2]
    factor = (head_scale / math.sqrt(head_dim))[:, None]
    queries = (factor * unit_rms(query_raw)).astype(jnp.bfloat16)
    keys = unit_rms(key_raw).astype(jnp.bfloat16)
    values = value_raw.astype(jnp.bfloat16)
    both_all = lon_gather(
        jnp.concatenate(
            [
                keys.reshape(lat_local, lon_local, channels),
                values.reshape(lat_local, lon_local, channels),
            ],
            axis=-1,
        )
    )
    key_all, value_all = both_all[..., :channels], both_all[..., channels:]
    lon_total = key_all.shape[1]
    key_heads = key_all.reshape(lat_local, lon_total, HEADS, head_dim)
    value_heads = value_all.reshape(lat_local, lon_total, HEADS, head_dim)
    scores = jnp.einsum("aihd,ajhd->ahij", queries, key_heads, preferred_element_type=jnp.float32)
    row_max = jnp.max(scores, axis=-1)
    exponent = jnp.exp(scores - row_max[..., None])
    row_sum = jnp.sum(exponent, axis=-1)
    weights_exp = exponent.astype(jnp.bfloat16)
    mixed = jnp.einsum(
        "ahij,ajhd->aihd", weights_exp, value_heads, preferred_element_type=jnp.float32
    )
    mixed = (mixed / row_sum.transpose(0, 2, 1)[..., None]).astype(jnp.bfloat16)
    attended = jnp.dot(mixed.reshape(-1, channels), project_out, preferred_element_type=jnp.float32)
    hidden = (source + attended.reshape(lat_local, lon_local, channels)).astype(jnp.bfloat16)
    hidden_wide = hidden.astype(jnp.float32)
    block_in = layer_norm(hidden_wide, convolve_gain).astype(jnp.bfloat16)
    paired = widen(jnp.concatenate([block_in, cotangent], axis=-1), 1)
    first = convolve(paired[..., :channels], filter_one, lat_local, lon_local, False)
    active = smooth(first).astype(jnp.bfloat16)
    second = convolve(widen(active, 1), filter_two, lat_local, lon_local, False)
    output = (hidden_wide + second).astype(jnp.bfloat16)
    d_active = convolve(paired[..., channels:], filter_two, lat_local, lon_local, True)
    d_first = (d_active * smooth_slope(first)).astype(jnp.bfloat16)
    d_block = convolve(widen(d_first, 1), filter_one, lat_local, lon_local, True)
    d_hidden = (
        cotangent.astype(jnp.float32) + layer_norm_back(hidden_wide, convolve_gain, d_block)
    ).astype(jnp.bfloat16)
    d_mixed = jnp.dot(
        d_hidden.reshape(-1, channels), project_out.T, preferred_element_type=jnp.float32
    )
    d_mixed = d_mixed.astype(jnp.bfloat16).reshape(lat_local, lon_local, HEADS, head_dim)
    probs = exponent / row_sum[..., None]
    probs_b = probs.astype(jnp.bfloat16)
    slope = jnp.einsum("aihd,ajhd->ahij", d_mixed, value_heads, preferred_element_type=jnp.float32)
    inner = jnp.sum(d_mixed.astype(jnp.float32) * mixed.astype(jnp.float32), axis=-1).transpose(
        0, 2, 1
    )
    d_score = (probs * (slope - inner[..., None])).astype(jnp.bfloat16)
    d_query = jnp.einsum("ahij,ajhd->aihd", d_score, key_heads, preferred_element_type=jnp.float32)
    count = lon_local * lax.axis_size(LON)
    key_term = jnp.einsum("ahij,aihd->jahd", d_score, queries, preferred_element_type=jnp.float32)
    value_term = jnp.einsum("ahij,aihd->jahd", probs_b, d_mixed, preferred_element_type=jnp.float32)
    summed = lon_reduce(
        jnp.concatenate(
            [
                key_term.reshape(count, lat_local, channels),
                value_term.reshape(count, lat_local, channels),
            ],
            axis=-1,
        )
    ).transpose(1, 0, 2)
    d_key = summed[..., :channels].reshape(lat_local, lon_local, HEADS, head_dim)
    d_value = summed[..., channels:].reshape(lat_local, lon_local, HEADS, head_dim)
    d_query_raw = unit_rms_back(query_raw, factor * d_query)
    d_key_raw = unit_rms_back(key_raw, d_key)
    d_proj = (
        jnp.stack([d_query_raw, d_key_raw, d_value], axis=2)
        .astype(jnp.bfloat16)
        .reshape(-1, 3 * channels)
    )
    d_normed = jnp.dot(d_proj, project_in.T, preferred_element_type=jnp.float32).reshape(
        lat_local, lon_local, channels
    )
    d_weather = (
        d_hidden.astype(jnp.float32) + layer_norm_back(source, attend_gain, d_normed)
    ).astype(jnp.bfloat16)
    return (output, d_weather)


def solution(mesh):
    fine = Mesh(mesh.devices.reshape(FINE), LAT + LON)
    placed = (
        P(LAT, LON, None),
        P(LAT, LON, None),
        P(),
        P(),
        P(),
        P(),
        P(),
        P(None, LAT, None),
        P(None, LAT, None),
    )
    return jax.shard_map(
        shards,
        mesh=fine,
        in_specs=placed,
        out_specs=(P(LAT, LON, None), P(LAT, LON, None)),
        check_vma=False,
    )
```

```python
import math

import jax
import jax.numpy as jnp
from jax import lax
from jax.sharding import Mesh, PartitionSpec as P

HEADS = 8
LAT = ("z", "x", "y_lo")
LON = ("y_hi", "core")
FINE = (8, 4, 2, 2, 2)


def ring_gather(block, axis, count, dim, split=False):
    forward = [(i, (i + 1) % count) for i in range(count)]
    backward = [(i, (i - 1) % count) for i in range(count)]
    relative = [block] + [None] * (count - 1)
    ahead, behind = block, block
    for step in range(1, count // 2 + 1):
        if step == count - step and split:
            half = block.shape[-1] // 2
            near = lax.ppermute(ahead[..., :half], axis, forward)
            far = lax.ppermute(behind[..., half:], axis, backward)
            relative[step] = jnp.concatenate([near, far], axis=-1)
            continue
        ahead = lax.ppermute(ahead, axis, forward)
        relative[count - step] = ahead
        if step < count - step:
            behind = lax.ppermute(behind, axis, backward)
            relative[step] = behind
    return jnp.stack(relative, axis=dim)


def swap(block, axis):
    return lax.ppermute(block, axis, [(0, 1), (1, 0)])


def lon_gather(block):
    core = lax.axis_index("core") == 0
    upper = lax.axis_index("y_hi") == 0
    far = swap(block, "y_hi")
    pair = jnp.stack([jnp.where(upper, block, far), jnp.where(upper, far, block)])
    other = swap(pair, "core")
    low, high = jnp.where(core, pair, other), jnp.where(core, other, pair)
    return jnp.concatenate([low[0], high[0], low[1], high[1]], axis=1)


def lon_reduce(total, dim):
    core = lax.axis_index("core") == 0
    upper = lax.axis_index("y_hi") == 0
    blocks = total.reshape(*total.shape[:dim], 2, 2, -1, *total.shape[dim + 1 :])
    pick = lambda array, axis, index: lax.index_in_dim(array, index, axis, keepdims=False)
    keep = jnp.where(core, pick(blocks, dim + 1, 0), pick(blocks, dim + 1, 1))
    send = jnp.where(core, pick(blocks, dim + 1, 1), pick(blocks, dim + 1, 0))
    part = keep + swap(send.astype(jnp.bfloat16), "core").astype(jnp.float32)
    keep = jnp.where(upper, pick(part, dim, 0), pick(part, dim, 1))
    send = jnp.where(upper, pick(part, dim, 1), pick(part, dim, 0))
    return keep + swap(send.astype(jnp.bfloat16), "y_hi").astype(jnp.float32)


def gather_filters(conv_first, conv_second):
    taps, rows, width = conv_first.shape
    half = width // 2
    core = lax.axis_index("core")
    both = jnp.stack([conv_first, conv_second])
    mine = lax.dynamic_slice_in_dim(both, core * half, half, axis=3)
    mine = ring_gather(mine, "y_lo", 2, 2)
    mine = ring_gather(mine, "z", 8, 2)
    mine = ring_gather(mine, "x", 4, 3, True)
    mine = mine.reshape(2, taps, -1, half)
    other = lax.ppermute(mine, "core", [(0, 1), (1, 0)])
    return (mine[0], other[0]), (mine[1], other[1])


def turn(width, rows):
    place = jnp.arange(width)
    local = place % rows
    block = place // rows
    ring_y = block % 2
    ring_x = (block // 2) % 4
    ring_z = block // 8
    true_z = (ring_z + lax.axis_index("z")) % 8
    true_x = (ring_x + lax.axis_index("x")) % 4
    true_y = (ring_y + lax.axis_index("y_lo")) % 2
    source = ((true_z * 4 + true_x) * 2 + true_y) * rows + local
    return (place[:, None] == source[None, :]).astype(jnp.bfloat16)


def with_halo(block, sides, width, periodic):
    for axis, dim in sides:
        count = lax.axis_size(axis)
        forward = [(i, i + 1) for i in range(count - 1)]
        if periodic:
            forward.append((count - 1, 0))
        backward = [(target, source) for source, target in forward]
        low = lax.ppermute(
            lax.slice_in_dim(block, block.shape[dim] - width, None, axis=dim), axis, forward
        )
        high = lax.ppermute(lax.slice_in_dim(block, 0, width, axis=dim), axis, backward)
        block = jnp.concatenate([low, block, high], axis=dim)
    return block


def layer_norm(values, channel_gain):
    center = values - jnp.mean(values, axis=-1, keepdims=True)
    spread = jnp.mean(center * center, axis=-1, keepdims=True)
    return center * lax.rsqrt(spread + 1e-05) * channel_gain


def layer_norm_back(values, channel_gain, upstream):
    _, pullback = jax.vjp(lambda argument: layer_norm(argument, channel_gain), values)
    return pullback(upstream)[0]


def unit_rms(values):
    return values * lax.rsqrt(jnp.mean(values * values, axis=-1, keepdims=True) + 1e-06)


def unit_rms_back(values, upstream):
    _, pullback = jax.vjp(unit_rms, values)
    return pullback(upstream)[0]


def smooth(values):
    return jax.nn.gelu(values, approximate=True)


def smooth_slope(values):
    _, pullback = jax.vjp(smooth, values)
    return pullback(jnp.ones_like(values))[0]


def convolve(padded, weight, row_count, col_count, flipped):
    channels = padded.shape[-1]
    mine, other = weight
    half = mine.shape[-1]
    first = lax.axis_index("core") == 0
    rows = channels // 64
    permute = turn(channels, rows)
    if not flipped:
        padded = jnp.dot(padded, permute, preferred_element_type=jnp.float32).astype(padded.dtype)
    if flipped:
        start = lax.axis_index("core") * half
        own = lax.dynamic_slice_in_dim(padded, start, half, axis=2)
        rest = lax.dynamic_slice_in_dim(padded, half - start, half, axis=2)
        summed = jnp.zeros((row_count * col_count, channels), jnp.float32)
    else:
        summed_mine = jnp.zeros((row_count * col_count, half), jnp.float32)
        summed_other = jnp.zeros((row_count * col_count, half), jnp.float32)
    for offset in range(9):
        upward, sideways = divmod(offset, 3)
        if flipped:
            start_row, start_col = (2 - upward, 2 - sideways)
            for source, kernel in ((own, mine), (rest, other)):
                window = source[
                    start_row : start_row + row_count, start_col : start_col + col_count
                ].reshape(row_count * col_count, half)
                summed = summed + jnp.dot(
                    window, kernel[offset].T, preferred_element_type=jnp.float32
                )
        else:
            window = padded[
                upward : upward + row_count, sideways : sideways + col_count
            ].reshape(row_count * col_count, channels)
            summed_mine = summed_mine + jnp.dot(
                window, mine[offset], preferred_element_type=jnp.float32
            )
            summed_other = summed_other + jnp.dot(
                window, other[offset], preferred_element_type=jnp.float32
            )
    if not flipped:
        summed = jnp.where(
            first,
            jnp.concatenate([summed_mine, summed_other], axis=-1),
            jnp.concatenate([summed_other, summed_mine], axis=-1),
        )
    else:
        summed = jnp.dot(
            summed, permute.astype(jnp.float32).T, precision=lax.Precision.HIGHEST
        )
    return summed.reshape(row_count, col_count, -1)


def widen(values, margin):
    banded = with_halo(values, ((LAT, 0),), margin, False)
    return with_halo(banded, ((LON, 1),), margin, True)


def shards(
    weather,
    cotangent,
    attend_gain,
    project_in,
    head_scale,
    project_out,
    convolve_gain,
    conv_first,
    conv_second,
):
    lat_local, lon_local, channels = weather.shape
    head_dim = channels // HEADS
    filter_one, filter_two = gather_filters(conv_first, conv_second)
    source = weather.astype(jnp.float32)
    normed = layer_norm(source, attend_gain).astype(jnp.bfloat16)
    projected = jnp.dot(
        normed.reshape(-1, channels), project_in, preferred_element_type=jnp.float32
    )
    projected = projected.reshape(lat_local, lon_local, 3, HEADS, head_dim)
    query_raw = projected[:, :, 0]
    key_raw = projected[:, :, 1]
    value_raw = projected[:, :, 2]
    factor = (head_scale / math.sqrt(head_dim))[:, None]
    queries = (factor * unit_rms(query_raw)).astype(jnp.bfloat16)
    keys = unit_rms(key_raw).astype(jnp.bfloat16)
    values = value_raw.astype(jnp.bfloat16)
    both_all = lon_gather(
        jnp.concatenate(
            [
                keys.reshape(lat_local, lon_local, channels),
                values.reshape(lat_local, lon_local, channels),
            ],
            axis=-1,
        )
    )
    key_all, value_all = both_all[..., :channels], both_all[..., channels:]
    lon_total = key_all.shape[1]
    key_heads = key_all.reshape(lat_local, lon_total, HEADS, head_dim)
    value_heads = value_all.reshape(lat_local, lon_total, HEADS, head_dim)
    scores = jnp.einsum("aihd,ajhd->ahij", queries, key_heads, preferred_element_type=jnp.float32)
    row_max = jnp.max(scores, axis=-1)
    exponent = jnp.exp(scores - row_max[..., None])
    row_sum = jnp.sum(exponent, axis=-1)
    weights_exp = exponent.astype(jnp.bfloat16)
    mixed = jnp.einsum(
        "ahij,ajhd->aihd", weights_exp, value_heads, preferred_element_type=jnp.float32
    )
    mixed = (mixed / row_sum.transpose(0, 2, 1)[..., None]).astype(jnp.bfloat16)
    attended = jnp.dot(mixed.reshape(-1, channels), project_out, preferred_element_type=jnp.float32)
    hidden = (source + attended.reshape(lat_local, lon_local, channels)).astype(jnp.bfloat16)
    hidden_wide = hidden.astype(jnp.float32)
    block_in = layer_norm(hidden_wide, convolve_gain).astype(jnp.bfloat16)
    paired = widen(jnp.concatenate([block_in, cotangent], axis=-1), 1)
    first = convolve(paired[..., :channels], filter_one, lat_local, lon_local, False)
    active = smooth(first).astype(jnp.bfloat16)
    second = convolve(widen(active, 1), filter_two, lat_local, lon_local, False)
    output = (hidden_wide + second).astype(jnp.bfloat16)
    d_active = convolve(paired[..., channels:], filter_two, lat_local, lon_local, True)
    d_first = (d_active * smooth_slope(first)).astype(jnp.bfloat16)
    d_block = convolve(widen(d_first, 1), filter_one, lat_local, lon_local, True)
    d_hidden = (
        cotangent.astype(jnp.float32) + layer_norm_back(hidden_wide, convolve_gain, d_block)
    ).astype(jnp.bfloat16)
    d_mixed = jnp.dot(
        d_hidden.reshape(-1, channels), project_out.T, preferred_element_type=jnp.float32
    )
    d_mixed = d_mixed.astype(jnp.bfloat16).reshape(lat_local, lon_local, HEADS, head_dim)
    probs = exponent / row_sum[..., None]
    probs_b = probs.astype(jnp.bfloat16)
    slope = jnp.einsum("aihd,ajhd->ahij", d_mixed, value_heads, preferred_element_type=jnp.float32)
    inner = jnp.sum(d_mixed.astype(jnp.float32) * mixed.astype(jnp.float32), axis=-1).transpose(
        0, 2, 1
    )
    d_score = (probs * (slope - inner[..., None])).astype(jnp.bfloat16)
    d_query = jnp.einsum("ahij,ajhd->aihd", d_score, key_heads, preferred_element_type=jnp.float32)
    key_term = jnp.einsum("ahij,aihd->ahjd", d_score, queries, preferred_element_type=jnp.float32)
    value_term = jnp.einsum("ahij,aihd->ahjd", probs_b, d_mixed, preferred_element_type=jnp.float32)
    summed = lon_reduce(jnp.stack([key_term, value_term]), 3).transpose(0, 1, 3, 2, 4)
    d_key, d_value = summed[0], summed[1]
    d_query_raw = unit_rms_back(query_raw, factor * d_query)
    d_key_raw = unit_rms_back(key_raw, d_key)
    d_proj = (
        jnp.stack([d_query_raw, d_key_raw, d_value], axis=2)
        .astype(jnp.bfloat16)
        .reshape(-1, 3 * channels)
    )
    d_normed = jnp.dot(d_proj, project_in.T, preferred_element_type=jnp.float32).reshape(
        lat_local, lon_local, channels
    )
    d_weather = (
        d_hidden.astype(jnp.float32) + layer_norm_back(source, attend_gain, d_normed)
    ).astype(jnp.bfloat16)
    return (output, d_weather)


def solution(mesh):
    fine = Mesh(mesh.devices.reshape(FINE), LAT + LON)
    placed = (
        P(LAT, LON, None),
        P(LAT, LON, None),
        P(),
        P(),
        P(),
        P(),
        P(),
        P(None, LAT, None),
        P(None, LAT, None),
    )
    return jax.shard_map(
        shards,
        mesh=fine,
        in_specs=placed,
        out_specs=(P(LAT, LON, None), P(LAT, LON, None)),
        check_vma=False,
    )
```

```python
import math

import jax
import jax.numpy as jnp
from jax import lax
from jax.sharding import Mesh, PartitionSpec as P

HEADS = 8
LAT = ("z", "x", "y_lo")
LON = ("y_hi", "core")
FINE = (8, 4, 2, 2, 2)


def ring_gather(block, axis, count, dim, split=False):
    forward = [(i, (i + 1) % count) for i in range(count)]
    backward = [(i, (i - 1) % count) for i in range(count)]
    relative = [block] + [None] * (count - 1)
    ahead, behind = block, block
    for step in range(1, count // 2 + 1):
        if step == count - step and split:
            half = block.shape[-1] // 2
            near = lax.ppermute(ahead[..., :half], axis, forward)
            far = lax.ppermute(behind[..., half:], axis, backward)
            relative[step] = jnp.concatenate([near, far], axis=-1)
            continue
        ahead = lax.ppermute(ahead, axis, forward)
        relative[count - step] = ahead
        if step < count - step:
            behind = lax.ppermute(behind, axis, backward)
            relative[step] = behind
    return jnp.stack(relative, axis=dim)


def swap(block, axis):
    return lax.ppermute(block, axis, [(0, 1), (1, 0)])


def lon_gather(block):
    core = lax.axis_index("core") == 0
    upper = lax.axis_index("y_hi") == 0
    far = swap(block, "y_hi")
    pair = jnp.stack([jnp.where(upper, block, far), jnp.where(upper, far, block)])
    other = swap(pair, "core")
    low, high = jnp.where(core, pair, other), jnp.where(core, other, pair)
    return jnp.concatenate([low[0], high[0], low[1], high[1]], axis=1)


def lon_reduce(total):
    core = lax.axis_index("core") == 0
    upper = lax.axis_index("y_hi") == 0
    blocks = total.reshape(2, 2, -1, *total.shape[1:])
    keep = jnp.where(core, blocks[:, 0], blocks[:, 1])
    send = jnp.where(core, blocks[:, 1], blocks[:, 0])
    part = keep + swap(send.astype(jnp.bfloat16), "core").astype(jnp.float32)
    keep = jnp.where(upper, part[0], part[1])
    send = jnp.where(upper, part[1], part[0])
    return keep + swap(send.astype(jnp.bfloat16), "y_hi").astype(jnp.float32)


def gather_filters(conv_first, conv_second):
    taps, rows, width = conv_first.shape
    half = width // 2
    core = lax.axis_index("core")
    both = jnp.stack([conv_first, conv_second])
    mine = lax.dynamic_slice_in_dim(both, core * half, half, axis=3)
    mine = ring_gather(mine, "y_lo", 2, 2)
    mine = ring_gather(mine, "z", 8, 2)
    mine = ring_gather(mine, "x", 4, 3, True)
    mine = mine.reshape(2, taps, -1, half)
    other = [lax.ppermute(mine[w], "core", [(0, 1), (1, 0)]) for w in range(2)]
    return (mine[0], other[0]), (mine[1], other[1])


def turn(width, rows):
    place = jnp.arange(width)
    local = place % rows
    block = place // rows
    ring_y = block % 2
    ring_x = (block // 2) % 4
    ring_z = block // 8
    true_z = (ring_z + lax.axis_index("z")) % 8
    true_x = (ring_x + lax.axis_index("x")) % 4
    true_y = (ring_y + lax.axis_index("y_lo")) % 2
    source = ((true_z * 4 + true_x) * 2 + true_y) * rows + local
    return (place[:, None] == source[None, :]).astype(jnp.bfloat16)


def with_halo(block, sides, width, periodic):
    for axis, dim in sides:
        count = lax.axis_size(axis)
        forward = [(i, i + 1) for i in range(count - 1)]
        if periodic:
            forward.append((count - 1, 0))
        backward = [(target, source) for source, target in forward]
        low = lax.ppermute(
            lax.slice_in_dim(block, block.shape[dim] - width, None, axis=dim), axis, forward
        )
        high = lax.ppermute(lax.slice_in_dim(block, 0, width, axis=dim), axis, backward)
        block = jnp.concatenate([low, block, high], axis=dim)
    return block


def layer_norm(values, channel_gain):
    center = values - jnp.mean(values, axis=-1, keepdims=True)
    spread = jnp.mean(center * center, axis=-1, keepdims=True)
    return center * lax.rsqrt(spread + 1e-05) * channel_gain


def layer_norm_back(values, channel_gain, upstream):
    _, pullback = jax.vjp(lambda argument: layer_norm(argument, channel_gain), values)
    return pullback(upstream)[0]


def unit_rms(values):
    return values * lax.rsqrt(jnp.mean(values * values, axis=-1, keepdims=True) + 1e-06)


def unit_rms_back(values, upstream):
    _, pullback = jax.vjp(unit_rms, values)
    return pullback(upstream)[0]


def smooth(values):
    return jax.nn.gelu(values, approximate=True)


def smooth_slope(values):
    _, pullback = jax.vjp(smooth, values)
    return pullback(jnp.ones_like(values))[0]


def convolve(padded, weight, row_count, col_count, flipped):
    channels = padded.shape[-1]
    mine, other = weight
    half = mine.shape[-1]
    first = lax.axis_index("core") == 0
    rows = channels // 64
    permute = turn(channels, rows)
    if not flipped:
        padded = jnp.dot(padded, permute, preferred_element_type=jnp.float32).astype(padded.dtype)
    if flipped:
        start = lax.axis_index("core") * half
        own = lax.dynamic_slice_in_dim(padded, start, half, axis=2)
        rest = lax.dynamic_slice_in_dim(padded, half - start, half, axis=2)
        summed = jnp.zeros((row_count * col_count, channels), jnp.float32)
    else:
        summed_mine = jnp.zeros((row_count * col_count, half), jnp.float32)
        summed_other = jnp.zeros((row_count * col_count, half), jnp.float32)
    for offset in range(9):
        upward, sideways = divmod(offset, 3)
        if flipped:
            start_row, start_col = (2 - upward, 2 - sideways)
            for source, kernel in ((own, mine), (rest, other)):
                window = source[
                    start_row : start_row + row_count, start_col : start_col + col_count
                ].reshape(row_count * col_count, half)
                summed = summed + jnp.dot(
                    window, kernel[offset].T, preferred_element_type=jnp.float32
                )
        else:
            window = padded[
                upward : upward + row_count, sideways : sideways + col_count
            ].reshape(row_count * col_count, channels)
            summed_mine = summed_mine + jnp.dot(
                window, mine[offset], preferred_element_type=jnp.float32
            )
            summed_other = summed_other + jnp.dot(
                window, other[offset], preferred_element_type=jnp.float32
            )
    if not flipped:
        summed = jnp.where(
            first,
            jnp.concatenate([summed_mine, summed_other], axis=-1),
            jnp.concatenate([summed_other, summed_mine], axis=-1),
        )
    else:
        summed = jnp.dot(
            summed, permute.astype(jnp.float32).T, precision=lax.Precision.HIGHEST
        )
    return summed.reshape(row_count, col_count, -1)


def widen(values, margin):
    banded = with_halo(values, ((LAT, 0),), margin, False)
    return with_halo(banded, ((LON, 1),), margin, True)


def shards(
    weather,
    cotangent,
    attend_gain,
    project_in,
    head_scale,
    project_out,
    convolve_gain,
    conv_first,
    conv_second,
):
    lat_local, lon_local, channels = weather.shape
    head_dim = channels // HEADS
    filter_one, filter_two = gather_filters(conv_first, conv_second)
    source = weather.astype(jnp.float32)
    normed = layer_norm(source, attend_gain).astype(jnp.bfloat16)
    projected = jnp.dot(
        normed.reshape(-1, channels), project_in, preferred_element_type=jnp.float32
    )
    projected = projected.reshape(lat_local, lon_local, 3, HEADS, head_dim)
    query_raw = projected[:, :, 0]
    key_raw = projected[:, :, 1]
    value_raw = projected[:, :, 2]
    factor = (head_scale / math.sqrt(head_dim))[:, None]
    queries = (factor * unit_rms(query_raw)).astype(jnp.bfloat16)
    keys = unit_rms(key_raw).astype(jnp.bfloat16)
    values = value_raw.astype(jnp.bfloat16)
    both_all = lon_gather(
        jnp.concatenate(
            [
                keys.reshape(lat_local, lon_local, channels),
                values.reshape(lat_local, lon_local, channels),
            ],
            axis=-1,
        )
    )
    key_all, value_all = both_all[..., :channels], both_all[..., channels:]
    lon_total = key_all.shape[1]
    key_heads = key_all.reshape(lat_local, lon_total, HEADS, head_dim)
    value_heads = value_all.reshape(lat_local, lon_total, HEADS, head_dim)
    scores = jnp.einsum("aihd,ajhd->ahij", queries, key_heads, preferred_element_type=jnp.float32)
    row_max = jnp.max(scores, axis=-1)
    exponent = jnp.exp(scores - row_max[..., None])
    row_sum = jnp.sum(exponent, axis=-1)
    weights_exp = exponent.astype(jnp.bfloat16)
    mixed = jnp.einsum(
        "ahij,ajhd->aihd", weights_exp, value_heads, preferred_element_type=jnp.float32
    )
    mixed = (mixed / row_sum.transpose(0, 2, 1)[..., None]).astype(jnp.bfloat16)
    attended = jnp.dot(mixed.reshape(-1, channels), project_out, preferred_element_type=jnp.float32)
    hidden = (source + attended.reshape(lat_local, lon_local, channels)).astype(jnp.bfloat16)
    hidden_wide = hidden.astype(jnp.float32)
    block_in = layer_norm(hidden_wide, convolve_gain).astype(jnp.bfloat16)
    paired = widen(jnp.concatenate([block_in, cotangent], axis=-1), 1)
    first = convolve(paired[..., :channels], filter_one, lat_local, lon_local, False)
    active = smooth(first).astype(jnp.bfloat16)
    second = convolve(widen(active, 1), filter_two, lat_local, lon_local, False)
    output = (hidden_wide + second).astype(jnp.bfloat16)
    d_active = convolve(paired[..., channels:], filter_two, lat_local, lon_local, True)
    d_first = (d_active * smooth_slope(first)).astype(jnp.bfloat16)
    d_block = convolve(widen(d_first, 1), filter_one, lat_local, lon_local, True)
    d_hidden = (
        cotangent.astype(jnp.float32) + layer_norm_back(hidden_wide, convolve_gain, d_block)
    ).astype(jnp.bfloat16)
    d_mixed = jnp.dot(
        d_hidden.reshape(-1, channels), project_out.T, preferred_element_type=jnp.float32
    )
    d_mixed = d_mixed.astype(jnp.bfloat16).reshape(lat_local, lon_local, HEADS, head_dim)
    probs = exponent / row_sum[..., None]
    probs_b = probs.astype(jnp.bfloat16)
    slope = jnp.einsum("aihd,ajhd->ahij", d_mixed, value_heads, preferred_element_type=jnp.float32)
    inner = jnp.sum(d_mixed.astype(jnp.float32) * mixed.astype(jnp.float32), axis=-1).transpose(
        0, 2, 1
    )
    d_score = (probs * (slope - inner[..., None])).astype(jnp.bfloat16)
    d_query = jnp.einsum("ahij,ajhd->aihd", d_score, key_heads, preferred_element_type=jnp.float32)
    count = lon_local * lax.axis_size(LON)
    key_term = jnp.einsum("ahij,aihd->jahd", d_score, queries, preferred_element_type=jnp.float32)
    value_term = jnp.einsum("ahij,aihd->jahd", probs_b, d_mixed, preferred_element_type=jnp.float32)
    summed = lon_reduce(
        jnp.concatenate(
            [
                key_term.reshape(count, lat_local, channels),
                value_term.reshape(count, lat_local, channels),
            ],
            axis=-1,
        )
    ).transpose(1, 0, 2)
    d_key = summed[..., :channels].reshape(lat_local, lon_local, HEADS, head_dim)
    d_value = summed[..., channels:].reshape(lat_local, lon_local, HEADS, head_dim)
    d_query_raw = unit_rms_back(query_raw, factor * d_query)
    d_key_raw = unit_rms_back(key_raw, d_key)
    d_proj = (
        jnp.stack([d_query_raw, d_key_raw, d_value], axis=2)
        .astype(jnp.bfloat16)
        .reshape(-1, 3 * channels)
    )
    d_normed = jnp.dot(d_proj, project_in.T, preferred_element_type=jnp.float32).reshape(
        lat_local, lon_local, channels
    )
    d_weather = (
        d_hidden.astype(jnp.float32) + layer_norm_back(source, attend_gain, d_normed)
    ).astype(jnp.bfloat16)
    return (output, d_weather)


def solution(mesh):
    fine = Mesh(mesh.devices.reshape(FINE), LAT + LON)
    placed = (
        P(LAT, LON, None),
        P(LAT, LON, None),
        P(),
        P(),
        P(),
        P(),
        P(),
        P(None, LAT, None),
        P(None, LAT, None),
    )
    return jax.shard_map(
        shards,
        mesh=fine,
        in_specs=placed,
        out_specs=(P(LAT, LON, None), P(LAT, LON, None)),
        check_vma=False,
    )
```
